128 devices in a mesh: row: 8 (over z, core), col: 8 (over y_hi, x), dp: 2 (over y_lo).
Axes of the slice: x: 4, y: 4 (y_hi: 2, y_lo: 2; y = y_hi * 2 + y_lo), z: 4, core: 2. Of those that a mesh axis runs over, the one named last changes fastest.
Arguments:
- tokens: bfloat16 [2048, 4096], P(('col', 'dp'), 'row'), may hold values from -6 to 6
- timesteps: int32 [8], replicated, may hold values from 0 to 999
- ada_weight: bfloat16 [3, 4096, 4096], P(None, 'col', 'row'), may hold values from -0.09375 to 0.09375
- up_weight: bfloat16 [4096, 16384], P('row', 'col'), may hold values from -0.90625 to 0.90625
- down_weight: bfloat16 [16384, 4096], P('col', 'row'), may hold values from -0.046875 to 0.046875
- cotangent: bfloat16 [2048, 4096], P(('col', 'dp'), 'row'), may hold values from -6 to 6
Outputs:
- grad_tokens: bfloat16 [2048, 4096], P(('col', 'dp'), 'row')
- grad_ada: float32 [3, 4096, 4096], P(None, 'col', 'row')
- grad_up: float32 [4096, 16384], P('row', ('col', 'dp'))
- grad_down: float32 [16384, 4096], P(('col', 'dp'), 'row')
The draws below stay inside these ranges and needn't reach their ends.
All inputs are finite; a program needn't handle non-finite values.
Results may differ from the reference program's by a relative error of at most 0.04.
Values may be sent and summed in bfloat16 or wider, within the bound.
No kernel may reach another device: no remote copies, remote signals or barrier semaphores. Data moves between devices by JAX's collectives and lax.ppermute only.
A program may use at most 128 MiB of HBM per device.

```python
import math
import jax
import jax.numpy as jnp
from jax import lax

D = 4096
FF = 16384
DB = 512
FB = 2048
VOL_TOK = 256
VOLS = 8
TOKENS = 2048
N_ROW = 8
N_COL = 8


def draw_up_weight(key, part):
    key_base = jax.random.fold_in(key, 11)
    key_noise = jax.random.fold_in(key_base, 1)
    key_common = jax.random.fold_in(key_base, 2)
    key_rough = jax.random.fold_in(key_base, 3)
    noise = jnp.clip(jax.random.normal(key_noise, (D, FF), jnp.float32), -6.0, 6.0)
    position = jnp.arange(D, dtype=jnp.float32) / (D - 1)
    rough = jax.random.uniform(key_rough, (D,), jnp.float32, 0.75, 1.25)
    rising = 0.5 + 1.5 * position
    common = jnp.clip(jax.random.normal(key_common, (FF,), jnp.float32), -4.0, 4.0)
    values = (noise + (rising * rough)[:, None] * common[None, :]) * D ** (-0.5)
    return values.astype(jnp.bfloat16)


def plant(drawn, key, smallest, top_value):
    longest = drawn.shape.index(max(drawn.shape))
    spots = []
    for shift in (0, 1):
        where = [jax.random.randint(jax.random.fold_in(key, axis), (), 0, length) for axis, length in enumerate(drawn.shape)]
        where[longest] = (where[longest] + shift) % drawn.shape[longest]
        spots.append(tuple(where))
    return drawn.at[spots[0]].set(smallest).at[spots[1]].set(top_value)


def shard_levels(stream_key, dims, split, smallest, largest):
    gain = 1.0
    for axis_at, parts in split:
        heights = jax.random.uniform(jax.random.fold_in(jax.random.fold_in(stream_key, 6), axis_at), (parts,), jnp.float32, smallest / len(split), largest / len(split))
        gain = gain * jnp.repeat(jnp.exp(heights), dims[axis_at] // parts).reshape((-1,) + (1,) * (len(dims) - 1 - axis_at))
    return gain


def scatter_about(rng, extent, spread, bound, shards=(), kind=jnp.bfloat16):
    result = spread * jax.random.normal(rng, extent, jnp.float32)
    if shards:
        result = result * shard_levels(rng, extent, shards, -0.22, 0.18)
    return jnp.clip(result, -bound, bound).astype(kind)


def setup_inputs(seed: int = 0) -> dict:
    keys = jax.random.split(jax.random.key(seed), 7)
    return {
        "tokens": scatter_about(keys[0], (TOKENS, D), 1.0, 6.0, ((0, 16), (1, 8))),
        "timesteps": plant(jax.random.randint(keys[1], (VOLS,), 0, 1000), jax.random.fold_in(keys[1], 1), 0, 999).astype(jnp.int32),
        "ada_weight": scatter_about(keys[2], (3, D, D), D ** -0.5, 0.09375, ((1, 8), (2, 8))),
        "up_weight": draw_up_weight(jax.random.fold_in(keys[6], 71), 0),
        "down_weight": scatter_about(keys[4], (FF, D), FF ** -0.5, 0.046875, ((0, 8), (1, 8))),
        "cotangent": scatter_about(keys[5], (TOKENS, D), 1.0, 6.0, ((0, 16), (1, 8))),
    }


tanh_scale = math.sqrt(2.0 / math.pi)

def gelu_tanh(h):
    return 0.5 * h * (1.0 + jnp.tanh(tanh_scale * (h + 0.044715 * h * h * h)))

def gelu_slope(h):
    inner = jnp.tanh(tanh_scale * (h + 0.044715 * h * h * h))
    return 0.5 * (1.0 + inner) + 0.5 * h * (1.0 - inner * inner) * tanh_scale * (1.0 + 3.0 * 0.044715 * h * h)

def time_features(timesteps, width):
    half = width // 2
    freqs = jnp.exp(-math.log(10000.0) * jnp.arange(half, dtype=jnp.float32) / half)
    angles = timesteps.astype(jnp.float32)[:, None] * freqs[None, :]
    embed = jnp.concatenate([jnp.cos(angles), jnp.sin(angles)], axis=1)
    return jax.nn.silu(embed).astype(jnp.bfloat16)

def rounded(value):
    return lax.optimization_barrier(value.astype(jnp.bfloat16)).astype(jnp.float32)

def reference(tokens, timesteps, ada_weight, up_weight, down_weight, cotangent):
    cond = time_features(timesteps, D)
    mod = jnp.einsum('vi,kio->vko', cond.astype(jnp.float32), ada_weight.astype(jnp.float32), precision=lax.Precision.HIGHEST)
    per_token = jnp.repeat(mod, VOL_TOK, axis=0)
    shift = per_token[:, 0]
    scale = per_token[:, 1]
    gate = per_token[:, 2]
    x = tokens.astype(jnp.float32)
    mean = lax.optimization_barrier(jnp.sum(x, axis=1)) / D
    var = lax.optimization_barrier(jnp.sum(x * x, axis=1)) / D - mean * mean
    rstd = lax.rsqrt(var + 1e-06)
    normed = (x - mean[:, None]) * rstd[:, None]
    modulated = (normed * (1.0 + scale) + shift).astype(jnp.bfloat16)
    hidden = jnp.zeros((TOKENS, FF), jnp.float32)
    for blk in range(N_ROW):
        part = jnp.dot(modulated[:, blk * DB:(blk + 1) * DB], up_weight[blk * DB:(blk + 1) * DB], preferred_element_type=jnp.float32)
        hidden = hidden + rounded(part)
    act = gelu_tanh(hidden).astype(jnp.bfloat16)
    branch = jnp.zeros((TOKENS, D), jnp.float32)
    for blk in range(N_COL):
        part = jnp.dot(act[:, blk * FB:(blk + 1) * FB], down_weight[blk * FB:(blk + 1) * FB], preferred_element_type=jnp.float32)
        branch = branch + rounded(part)
    cot = cotangent.astype(jnp.float32)
    grad_branch = (cot * gate).astype(jnp.bfloat16)
    grad_down = lax.dot_general(act, grad_branch, (((0,), (0,)), ((), ())), preferred_element_type=jnp.float32)
    grad_act = jnp.zeros((TOKENS, FF), jnp.float32)
    for blk in range(N_ROW):
        part = lax.dot_general(grad_branch[:, blk * DB:(blk + 1) * DB], down_weight[:, blk * DB:(blk + 1) * DB], (((1,), (1,)), ((), ())), preferred_element_type=jnp.float32)
        grad_act = grad_act + rounded(part)
    grad_hidden = (grad_act * gelu_slope(hidden)).astype(jnp.bfloat16)
    grad_up = lax.dot_general(modulated, grad_hidden, (((0,), (0,)), ((), ())), preferred_element_type=jnp.float32)
    grad_mod_in = jnp.zeros((TOKENS, D), jnp.float32)
    for blk in range(N_COL):
        part = lax.dot_general(grad_hidden[:, blk * FB:(blk + 1) * FB], up_weight[:, blk * FB:(blk + 1) * FB], (((1,), (1,)), ((), ())), preferred_element_type=jnp.float32)
        grad_mod_in = grad_mod_in + rounded(part)
    grad_shift = lax.optimization_barrier(jnp.sum(grad_mod_in.reshape(VOLS, VOL_TOK, D), axis=1))
    grad_scale = lax.optimization_barrier(jnp.sum((grad_mod_in * normed).reshape(VOLS, VOL_TOK, D), axis=1))
    grad_gate = lax.optimization_barrier(jnp.sum((cot * branch).reshape(VOLS, VOL_TOK, D), axis=1))
    grad_mod = jnp.stack([grad_shift, grad_scale, grad_gate], axis=1)
    grad_ada = jnp.einsum('vi,vko->kio', cond.astype(jnp.float32), grad_mod, precision=lax.Precision.HIGHEST)
    grad_norm = grad_mod_in * (1.0 + scale)
    first = lax.optimization_barrier(jnp.sum(grad_norm, axis=1)) / D
    second = lax.optimization_barrier(jnp.sum(grad_norm * normed, axis=1)) / D
    grad_tokens = cot + rstd[:, None] * (grad_norm - first[:, None] - normed * second[:, None])
    return (grad_tokens.astype(jnp.bfloat16), grad_ada, grad_up, grad_down)
```

```python
import math

import jax
import jax.numpy as jnp
from jax import lax
from jax.sharding import PartitionSpec as P

tanh_scale = math.sqrt(2.0 / math.pi)


def gelu_tanh(h):
    return 0.5 * h * (1.0 + jnp.tanh(tanh_scale * (h + 0.044715 * h * h * h)))


def gelu_slope(h):
    inner = jnp.tanh(tanh_scale * (h + 0.044715 * h * h * h))
    return 0.5 * (1.0 + inner) + 0.5 * h * (1.0 - inner * inner) * tanh_scale * (
        1.0 + 3.0 * 0.044715 * h * h
    )


def time_features(timesteps, width):
    half = width // 2
    freqs = jnp.exp(-math.log(10000.0) * jnp.arange(half, dtype=jnp.float32) / half)
    angles = timesteps.astype(jnp.float32)[:, None] * freqs[None, :]
    embed = jnp.concatenate([jnp.cos(angles), jnp.sin(angles)], axis=1)
    return jax.nn.silu(embed).astype(jnp.bfloat16)


def shifted(x, axis, n, s):
    return lax.ppermute(x, axis, [(j, (j + s) % n) for j in range(n)])


def slot_gather(x, axis, n):
    return jnp.concatenate([x] + [shifted(x, axis, n, s) for s in range(1, n)], axis=0)


def slot_scatter_sum(parts, axis, n):
    m = parts.shape[0] // n
    total = parts[0:m].astype(jnp.float32)
    for s in range(1, n):
        total = total + shifted(parts[s * m:(s + 1) * m], axis, n, -s).astype(jnp.float32)
    return total


def ring_sum(x, axis, n):
    total = x
    for s in range(1, n):
        total = total + shifted(x, axis, n, s)
    return total


def pair_scatter_sum(part, axis, dim):
    d = lax.axis_index(axis)
    half = part.shape[dim] // 2
    own = lax.dynamic_slice_in_dim(part, d * half, half, dim)
    other = lax.dynamic_slice_in_dim(part, (1 - d) * half, half, dim)
    got = lax.ppermute(other.astype(jnp.bfloat16), axis, [(0, 1), (1, 0)])
    return own + got.astype(jnp.float32)


def body(tokens, timesteps, ada_weight, up_weight, down_weight, cotangent):
    rows_count = lax.axis_size("row")
    cols_count = lax.axis_size("col")
    col_index = lax.axis_index("col")
    tok_rows, width = tokens.shape
    full_width = width * rows_count
    in_width = ada_weight.shape[1]
    cond = time_features(timesteps, full_width)
    cond_part = lax.dynamic_slice_in_dim(cond, col_index * in_width, in_width, 1)
    mod_terms = jnp.einsum("vi,kio->vko", cond_part, ada_weight, preferred_element_type=jnp.float32)
    own_mod = lax.dynamic_index_in_dim(mod_terms, col_index, 0, keepdims=False)
    for s in range(1, cols_count):
        piece = lax.dynamic_index_in_dim(mod_terms, (col_index + s) % cols_count, 0, keepdims=False)
        own_mod = own_mod + shifted(piece, "col", cols_count, s)
    shift = own_mod[0]
    scale = own_mod[1]
    gate = own_mod[2]
    x = tokens.astype(jnp.float32)
    stats = ring_sum(jnp.stack([jnp.sum(x, axis=1), jnp.sum(x * x, axis=1)], axis=0), "row", rows_count)
    mean = stats[0] / full_width
    var = stats[1] / full_width - mean * mean
    rstd = lax.rsqrt(var + 1e-06)
    normed = (x - mean[:, None]) * rstd[:, None]
    modulated = (normed * (1.0 + scale) + shift).astype(jnp.bfloat16)
    cot = cotangent.astype(jnp.float32)
    grad_branch = (cot * gate).astype(jnp.bfloat16)
    mod_full = slot_gather(modulated, "col", cols_count)
    branch_full = slot_gather(grad_branch, "col", cols_count)
    hidden_own = lax.psum_scatter(
        jnp.dot(mod_full, up_weight, preferred_element_type=jnp.float32).astype(jnp.bfloat16),
        "row",
        scatter_dimension=0,
        tiled=True,
    ).astype(jnp.float32)
    act_own = gelu_tanh(hidden_own).astype(jnp.bfloat16)
    act_full = lax.all_gather(act_own, "row", axis=0, tiled=True)
    branch = slot_scatter_sum(
        jnp.dot(act_full, down_weight, preferred_element_type=jnp.float32).astype(jnp.bfloat16),
        "col",
        cols_count,
    )
    grad_gate = jnp.sum(cot * branch, axis=0)
    down_part = lax.dot_general(
        act_full, branch_full, (((0,), (0,)), ((), ())), preferred_element_type=jnp.float32
    )
    grad_act = lax.psum_scatter(
        lax.dot_general(
            branch_full, down_weight, (((1,), (1,)), ((), ())), preferred_element_type=jnp.float32
        ).astype(jnp.bfloat16),
        "row",
        scatter_dimension=0,
        tiled=True,
    ).astype(jnp.float32)
    grad_hidden = (grad_act * gelu_slope(hidden_own)).astype(jnp.bfloat16)
    grad_full = lax.all_gather(grad_hidden, "row", axis=0, tiled=True)
    up_part = lax.dot_general(
        mod_full, grad_full, (((0,), (0,)), ((), ())), preferred_element_type=jnp.float32
    )
    grad_mod_in = slot_scatter_sum(
        lax.dot_general(
            grad_full, up_weight, (((1,), (1,)), ((), ())), preferred_element_type=jnp.float32
        ).astype(jnp.bfloat16),
        "col",
        cols_count,
    )
    grad_up = pair_scatter_sum(up_part, "dp", 1)
    grad_down = pair_scatter_sum(down_part, "dp", 0)
    grad_norm = grad_mod_in * (1.0 + scale)
    sums = ring_sum(
        jnp.stack([jnp.sum(grad_norm, axis=1), jnp.sum(grad_norm * normed, axis=1)], axis=0),
        "row",
        rows_count,
    )
    first = sums[0] / full_width
    second = sums[1] / full_width
    grad_tokens = cot + rstd[:, None] * (grad_norm - first[:, None] - normed * second[:, None])
    own_grad = jnp.stack(
        [jnp.sum(grad_mod_in, axis=0), jnp.sum(grad_mod_in * normed, axis=0), grad_gate], axis=0
    )
    vol_grad = own_grad + lax.ppermute(own_grad, "dp", [(0, 1), (1, 0)])
    grad_mod = jnp.stack(
        [vol_grad] + [shifted(vol_grad, "col", cols_count, s) for s in range(1, cols_count)], axis=0
    )
    slot_vol = (col_index - jnp.arange(cols_count, dtype=jnp.int32)) % cols_count
    cond_slots = jnp.take(cond_part.astype(jnp.float32), slot_vol, axis=0)
    grad_ada = jnp.einsum(
        "vi,vko->kio", cond_slots, grad_mod, precision=lax.Precision.HIGHEST
    )
    return (grad_tokens.astype(jnp.bfloat16), grad_ada, grad_up, grad_down)


def solution(mesh):
    return jax.shard_map(
        body,
        mesh=mesh,
        in_specs=(
            P(("col", "dp"), "row"),
            P(),
            P(None, "col", "row"),
            P("row", "col"),
            P("col", "row"),
            P(("col", "dp"), "row"),
        ),
        out_specs=(
            P(("col", "dp"), "row"),
            P(None, "col", "row"),
            P("row", ("col", "dp")),
            P(("col", "dp"), "row"),
        ),
        check_vma=False,
    )
```

```python
import math

import jax
import jax.numpy as jnp
from jax import lax
from jax.sharding import PartitionSpec as P

tanh_scale = math.sqrt(2.0 / math.pi)


def gelu_tanh(h):
    return 0.5 * h * (1.0 + jnp.tanh(tanh_scale * (h + 0.044715 * h * h * h)))


def gelu_slope(h):
    inner = jnp.tanh(tanh_scale * (h + 0.044715 * h * h * h))
    return 0.5 * (1.0 + inner) + 0.5 * h * (1.0 - inner * inner) * tanh_scale * (
        1.0 + 3.0 * 0.044715 * h * h
    )


def time_features(timesteps, width):
    half = width // 2
    freqs = jnp.exp(-math.log(10000.0) * jnp.arange(half, dtype=jnp.float32) / half)
    angles = timesteps.astype(jnp.float32)[:, None] * freqs[None, :]
    embed = jnp.concatenate([jnp.cos(angles), jnp.sin(angles)], axis=1)
    return jax.nn.silu(embed).astype(jnp.bfloat16)


def shifted(x, axis, n, s):
    return lax.ppermute(x, axis, [(j, (j + s) % n) for j in range(n)])


def col_gather(x, axis, n):
    rep = jnp.broadcast_to(x[None], (n,) + x.shape)
    got = lax.all_to_all(rep, axis, 0, 0, tiled=False)
    return got.reshape((n * x.shape[0],) + x.shape[1:])


def col_scatter_sum(parts, axis, n):
    m = parts.shape[0] // n
    got = lax.all_to_all(parts.reshape((n, m) + parts.shape[1:]), axis, 0, 0, tiled=False)
    return jnp.sum(got.astype(jnp.float32), axis=0)


def gather_sum(x, axis):
    return jnp.sum(lax.all_gather(x, axis, axis=0, tiled=False), axis=0)


def pair_scatter_sum(part, axis, dim):
    d = lax.axis_index(axis)
    half = part.shape[dim] // 2
    own = lax.dynamic_slice_in_dim(part, d * half, half, dim)
    other = lax.dynamic_slice_in_dim(part, (1 - d) * half, half, dim)
    got = lax.ppermute(other.astype(jnp.bfloat16), axis, [(0, 1), (1, 0)])
    return own + got.astype(jnp.float32)


def body(tokens, timesteps, ada_weight, up_weight, down_weight, cotangent):
    rows_count = lax.axis_size("row")
    cols_count = lax.axis_size("col")
    col_index = lax.axis_index("col")
    tok_rows, width = tokens.shape
    full_width = width * rows_count
    in_width = ada_weight.shape[1]
    cond = time_features(timesteps, full_width)
    cond_part = lax.dynamic_slice_in_dim(cond, col_index * in_width, in_width, 1)
    mod_terms = jnp.einsum("vi,kio->vko", cond_part, ada_weight, preferred_element_type=jnp.float32)
    own_mod = jnp.sum(lax.all_to_all(mod_terms, "col", 0, 0, tiled=False), axis=0)
    shift = own_mod[0]
    scale = own_mod[1]
    gate = own_mod[2]
    x = tokens.astype(jnp.float32)
    stats = gather_sum(jnp.stack([jnp.sum(x, axis=1), jnp.sum(x * x, axis=1)], axis=0), "row")
    mean = stats[0] / full_width
    var = stats[1] / full_width - mean * mean
    rstd = lax.rsqrt(var + 1e-06)
    normed = (x - mean[:, None]) * rstd[:, None]
    modulated = (normed * (1.0 + scale) + shift).astype(jnp.bfloat16)
    cot = cotangent.astype(jnp.float32)
    grad_branch = (cot * gate).astype(jnp.bfloat16)
    mod_full = col_gather(modulated, "col", cols_count)
    branch_full = col_gather(grad_branch, "col", cols_count)
    hidden_own = lax.psum_scatter(
        jnp.dot(mod_full, up_weight, preferred_element_type=jnp.float32).astype(jnp.bfloat16),
        "row",
        scatter_dimension=0,
        tiled=True,
    ).astype(jnp.float32)
    act_own = gelu_tanh(hidden_own).astype(jnp.bfloat16)
    act_full = lax.all_gather(act_own, "row", axis=0, tiled=True)
    branch = col_scatter_sum(
        jnp.dot(act_full, down_weight, preferred_element_type=jnp.float32).astype(jnp.bfloat16),
        "col",
        cols_count,
    )
    grad_gate = jnp.sum(cot * branch, axis=0)
    down_part = lax.dot_general(
        act_full, branch_full, (((0,), (0,)), ((), ())), preferred_element_type=jnp.float32
    )
    grad_act = lax.psum_scatter(
        lax.dot_general(
            branch_full, down_weight, (((1,), (1,)), ((), ())), preferred_element_type=jnp.float32
        ).astype(jnp.bfloat16),
        "row",
        scatter_dimension=0,
        tiled=True,
    ).astype(jnp.float32)
    grad_hidden = (grad_act * gelu_slope(hidden_own)).astype(jnp.bfloat16)
    grad_full = lax.all_gather(grad_hidden, "row", axis=0, tiled=True)
    up_part = lax.dot_general(
        mod_full, grad_full, (((0,), (0,)), ((), ())), preferred_element_type=jnp.float32
    )
    grad_mod_in = col_scatter_sum(
        lax.dot_general(
            grad_full, up_weight, (((1,), (1,)), ((), ())), preferred_element_type=jnp.float32
        ).astype(jnp.bfloat16),
        "col",
        cols_count,
    )
    grad_up = pair_scatter_sum(up_part, "dp", 1)
    grad_down = pair_scatter_sum(down_part, "dp", 0)
    grad_norm = grad_mod_in * (1.0 + scale)
    sums = gather_sum(
        jnp.stack([jnp.sum(grad_norm, axis=1), jnp.sum(grad_norm * normed, axis=1)], axis=0), "row"
    )
    first = sums[0] / full_width
    second = sums[1] / full_width
    grad_tokens = cot + rstd[:, None] * (grad_norm - first[:, None] - normed * second[:, None])
    own_grad = jnp.stack(
        [jnp.sum(grad_mod_in, axis=0), jnp.sum(grad_mod_in * normed, axis=0), grad_gate], axis=0
    )
    every_grad = lax.all_gather(own_grad, ("col", "dp"), axis=0, tiled=False)
    grad_mod = jnp.sum(every_grad.reshape((cols_count, -1) + own_grad.shape), axis=1)
    grad_ada = jnp.einsum(
        "vi,vko->kio", cond_part.astype(jnp.float32), grad_mod, precision=lax.Precision.HIGHEST
    )
    return (grad_tokens.astype(jnp.bfloat16), grad_ada, grad_up, grad_down)


def solution(mesh):
    return jax.shard_map(
        body,
        mesh=mesh,
        in_specs=(
            P(("col", "dp"), "row"),
            P(),
            P(None, "col", "row"),
            P("row", "col"),
            P("col", "row"),
            P(("col", "dp"), "row"),
        ),
        out_specs=(
            P(("col", "dp"), "row"),
            P(None, "col", "row"),
            P("row", ("col", "dp")),
            P(("col", "dp"), "row"),
        ),
        check_vma=False,
    )
```

```python
import math

import jax
import jax.numpy as jnp
from jax import lax
from jax.sharding import PartitionSpec as P

tanh_scale = math.sqrt(2.0 / math.pi)


def gelu_tanh(h):
    return 0.5 * h * (1.0 + jnp.tanh(tanh_scale * (h + 0.044715 * h * h * h)))


def gelu_slope(h):
    inner = jnp.tanh(tanh_scale * (h + 0.044715 * h * h * h))
    return 0.5 * (1.0 + inner) + 0.5 * h * (1.0 - inner * inner) * tanh_scale * (
        1.0 + 3.0 * 0.044715 * h * h
    )


def time_features(timesteps, width):
    half = width // 2
    freqs = jnp.exp(-math.log(10000.0) * jnp.arange(half, dtype=jnp.float32) / half)
    angles = timesteps.astype(jnp.float32)[:, None] * freqs[None, :]
    embed = jnp.concatenate([jnp.cos(angles), jnp.sin(angles)], axis=1)
    return jax.nn.silu(embed).astype(jnp.bfloat16)


def shifted(x, axis, n, s):
    return lax.ppermute(x, axis, [(j, (j + s) % n) for j in range(n)])


def slot_gather(x, axis, n):
    return jnp.concatenate([x] + [shifted(x, axis, n, s) for s in range(1, n)], axis=0)


def slot_scatter_sum(parts, axis, n):
    m = parts.shape[0] // n
    total = parts[0:m].astype(jnp.float32)
    for s in range(1, n):
        total = total + shifted(parts[s * m:(s + 1) * m], axis, n, -s).astype(jnp.float32)
    return total


def swapped(x, axis, n, m):
    return lax.ppermute(x, axis, [(j, j ^ m) for j in range(n)])


def ring_sum(x, axis, n):
    m = 1
    while m < n:
        x = x + swapped(x, axis, n, m)
        m *= 2
    return x


def halving_sum(x, axis, n):
    me = lax.axis_index(axis)
    m = n // 2
    while m >= 1:
        bit = (me // m) % 2
        keep = lax.dynamic_slice_in_dim(x, bit * m, m, 0)
        give = lax.dynamic_slice_in_dim(x, (1 - bit) * m, m, 0)
        x = keep + swapped(give, axis, n, m)
        m //= 2
    return x[0]


def pair_scatter_sum(part, axis, dim):
    d = lax.axis_index(axis)
    half = part.shape[dim] // 2
    own = lax.dynamic_slice_in_dim(part, d * half, half, dim)
    other = lax.dynamic_slice_in_dim(part, (1 - d) * half, half, dim)
    got = lax.ppermute(other.astype(jnp.bfloat16), axis, [(0, 1), (1, 0)])
    return own + got.astype(jnp.float32)


def body(tokens, timesteps, ada_weight, up_weight, down_weight, cotangent):
    rows_count = lax.axis_size("row")
    cols_count = lax.axis_size("col")
    col_index = lax.axis_index("col")
    tok_rows, width = tokens.shape
    full_width = width * rows_count
    in_width = ada_weight.shape[1]
    cond = time_features(timesteps, full_width)
    cond_part = lax.dynamic_slice_in_dim(cond, col_index * in_width, in_width, 1)
    mod_terms = jnp.einsum("vi,kio->vko", cond_part, ada_weight, preferred_element_type=jnp.float32)
    own_mod = halving_sum(mod_terms, "col", cols_count)
    shift = own_mod[0]
    scale = own_mod[1]
    gate = own_mod[2]
    x = tokens.astype(jnp.float32)
    stats = ring_sum(jnp.stack([jnp.sum(x, axis=1), jnp.sum(x * x, axis=1)], axis=0), "row", rows_count)
    mean = stats[0] / full_width
    var = stats[1] / full_width - mean * mean
    rstd = lax.rsqrt(var + 1e-06)
    normed = (x - mean[:, None]) * rstd[:, None]
    modulated = (normed * (1.0 + scale) + shift).astype(jnp.bfloat16)
    cot = cotangent.astype(jnp.float32)
    grad_branch = (cot * gate).astype(jnp.bfloat16)
    mod_full = slot_gather(modulated, "col", cols_count)
    branch_full = slot_gather(grad_branch, "col", cols_count)
    hidden_own = lax.psum_scatter(
        jnp.dot(mod_full, up_weight, preferred_element_type=jnp.float32).astype(jnp.bfloat16),
        "row",
        scatter_dimension=0,
        tiled=True,
    ).astype(jnp.float32)
    act_own = gelu_tanh(hidden_own).astype(jnp.bfloat16)
    act_full = lax.all_gather(act_own, "row", axis=0, tiled=True)
    branch = slot_scatter_sum(
        jnp.dot(act_full, down_weight, preferred_element_type=jnp.float32).astype(jnp.bfloat16),
        "col",
        cols_count,
    )
    grad_gate = jnp.sum(cot * branch, axis=0)
    down_part = lax.dot_general(
        act_full, branch_full, (((0,), (0,)), ((), ())), preferred_element_type=jnp.float32
    )
    grad_act = lax.psum_scatter(
        lax.dot_general(
            branch_full, down_weight, (((1,), (1,)), ((), ())), preferred_element_type=jnp.float32
        ).astype(jnp.bfloat16),
        "row",
        scatter_dimension=0,
        tiled=True,
    ).astype(jnp.float32)
    grad_hidden = (grad_act * gelu_slope(hidden_own)).astype(jnp.bfloat16)
    grad_full = lax.all_gather(grad_hidden, "row", axis=0, tiled=True)
    up_part = lax.dot_general(
        mod_full, grad_full, (((0,), (0,)), ((), ())), preferred_element_type=jnp.float32
    )
    grad_mod_in = slot_scatter_sum(
        lax.dot_general(
            grad_full, up_weight, (((1,), (1,)), ((), ())), preferred_element_type=jnp.float32
        ).astype(jnp.bfloat16),
        "col",
        cols_count,
    )
    grad_up = pair_scatter_sum(up_part, "dp", 1)
    grad_down = pair_scatter_sum(down_part, "dp", 0)
    grad_norm = grad_mod_in * (1.0 + scale)
    sums = ring_sum(
        jnp.stack([jnp.sum(grad_norm, axis=1), jnp.sum(grad_norm * normed, axis=1)], axis=0),
        "row",
        rows_count,
    )
    first = sums[0] / full_width
    second = sums[1] / full_width
    grad_tokens = cot + rstd[:, None] * (grad_norm - first[:, None] - normed * second[:, None])
    own_grad = jnp.stack(
        [jnp.sum(grad_mod_in, axis=0), jnp.sum(grad_mod_in * normed, axis=0), grad_gate], axis=0
    )
    placed = jnp.where(
        (jnp.arange(cols_count, dtype=jnp.int32) == col_index)[:, None, None], own_grad[None], 0.0
    )
    placed = placed + lax.ppermute(placed, "dp", [(0, 1), (1, 0)])
    grad_mod = ring_sum(placed, "col", cols_count)
    cond_f = cond_part.astype(jnp.float32)
    grad_ada = cond_f[0][None, :, None] * grad_mod[0][:, None, :]
    for v in range(1, cols_count):
        grad_ada = grad_ada + cond_f[v][None, :, None] * grad_mod[v][:, None, :]
    return (grad_tokens.astype(jnp.bfloat16), grad_ada, grad_up, grad_down)


def solution(mesh):
    return jax.shard_map(
        body,
        mesh=mesh,
        in_specs=(
            P(("col", "dp"), "row"),
            P(),
            P(None, "col", "row"),
            P("row", "col"),
            P("col", "row"),
            P(("col", "dp"), "row"),
        ),
        out_specs=(
            P(("col", "dp"), "row"),
            P(None, "col", "row"),
            P("row", ("col", "dp")),
            P(("col", "dp"), "row"),
        ),
        check_vma=False,
    )
```

```python
import math

import jax
import jax.numpy as jnp
from jax import lax
from jax.sharding import PartitionSpec as P

tanh_scale = math.sqrt(2.0 / math.pi)


def gelu_tanh(h):
    return 0.5 * h * (1.0 + jnp.tanh(tanh_scale * (h + 0.044715 * h * h * h)))


def gelu_slope(h):
    inner = jnp.tanh(tanh_scale * (h + 0.044715 * h * h * h))
    return 0.5 * (1.0 + inner) + 0.5 * h * (1.0 - inner * inner) * tanh_scale * (
        1.0 + 3.0 * 0.044715 * h * h
    )


def time_features(timesteps, width):
    half = width // 2
    freqs = jnp.exp(-math.log(10000.0) * jnp.arange(half, dtype=jnp.float32) / half)
    angles = timesteps.astype(jnp.float32)[:, None] * freqs[None, :]
    embed = jnp.concatenate([jnp.cos(angles), jnp.sin(angles)], axis=1)
    return jax.nn.silu(embed).astype(jnp.bfloat16)


def shifted(x, axis, n, s):
    return lax.ppermute(x, axis, [(j, (j + s) % n) for j in range(n)])


def slot_gather(x, axis, n):
    return jnp.concatenate([x] + [shifted(x, axis, n, s) for s in range(1, n)], axis=0)


def slot_scatter_sum(parts, axis, n):
    m = parts.shape[0] // n
    total = parts[0:m].astype(jnp.float32)
    for s in range(1, n):
        total = total + shifted(parts[s * m:(s + 1) * m], axis, n, -s).astype(jnp.float32)
    return total


def swapped(x, axis, n, m):
    return lax.ppermute(x, axis, [(j, j ^ m) for j in range(n)])


def ring_sum(x, axis, n):
    m = 1
    while m < n:
        x = x + swapped(x, axis, n, m)
        m *= 2
    return x


def halving_sum(x, axis, n):
    me = lax.axis_index(axis)
    m = n // 2
    while m >= 1:
        bit = (me // m) % 2
        keep = lax.dynamic_slice_in_dim(x, bit * m, m, 0)
        give = lax.dynamic_slice_in_dim(x, (1 - bit) * m, m, 0)
        x = keep + swapped(give, axis, n, m)
        m //= 2
    return x[0]


def pair_send(part, axis, dim):
    d = lax.axis_index(axis)
    half = part.shape[dim] // 2
    own = lax.dynamic_slice_in_dim(part, d * half, half, dim)
    other = lax.dynamic_slice_in_dim(part, (1 - d) * half, half, dim)
    got = lax.ppermute(other.astype(jnp.bfloat16), axis, [(0, 1), (1, 0)])
    return own, got


def body(tokens, timesteps, ada_weight, up_weight, down_weight, cotangent):
    rows_count = lax.axis_size("row")
    cols_count = lax.axis_size("col")
    col_index = lax.axis_index("col")
    tok_rows, width = tokens.shape
    full_width = width * rows_count
    in_width = ada_weight.shape[1]
    cond = time_features(timesteps, full_width)
    cond_part = lax.dynamic_slice_in_dim(cond, col_index * in_width, in_width, 1)
    mod_terms = jnp.einsum("vi,kio->vko", cond_part, ada_weight, preferred_element_type=jnp.float32)
    own_mod = halving_sum(mod_terms, "col", cols_count)
    shift = own_mod[0]
    scale = own_mod[1]
    gate = own_mod[2]
    x = tokens.astype(jnp.float32)
    stats = ring_sum(jnp.stack([jnp.sum(x, axis=1), jnp.sum(x * x, axis=1)], axis=0), "row", rows_count)
    mean = stats[0] / full_width
    var = stats[1] / full_width - mean * mean
    rstd = lax.rsqrt(var + 1e-06)
    normed = (x - mean[:, None]) * rstd[:, None]
    modulated = (normed * (1.0 + scale) + shift).astype(jnp.bfloat16)
    cot = cotangent.astype(jnp.float32)
    grad_branch = (cot * gate).astype(jnp.bfloat16)
    mod_full = slot_gather(modulated, "col", cols_count)
    branch_full = slot_gather(grad_branch, "col", cols_count)
    hidden_own = lax.psum_scatter(
        jnp.dot(mod_full, up_weight, preferred_element_type=jnp.float32).astype(jnp.bfloat16),
        "row",
        scatter_dimension=0,
        tiled=True,
    ).astype(jnp.float32)
    act_own = gelu_tanh(hidden_own).astype(jnp.bfloat16)
    act_full = lax.all_gather(act_own, "row", axis=0, tiled=True)
    branch = slot_scatter_sum(
        jnp.dot(act_full, down_weight, preferred_element_type=jnp.float32).astype(jnp.bfloat16),
        "col",
        cols_count,
    )
    grad_gate = jnp.sum(cot * branch, axis=0)
    down_part = lax.dot_general(
        act_full, branch_full, (((0,), (0,)), ((), ())), preferred_element_type=jnp.float32
    )
    grad_act = lax.psum_scatter(
        lax.dot_general(
            branch_full, down_weight, (((1,), (1,)), ((), ())), preferred_element_type=jnp.float32
        ).astype(jnp.bfloat16),
        "row",
        scatter_dimension=0,
        tiled=True,
    ).astype(jnp.float32)
    own_down, got_down = pair_send(down_part, "dp", 0)
    grad_hidden = (grad_act * gelu_slope(hidden_own)).astype(jnp.bfloat16)
    grad_full = lax.all_gather(grad_hidden, "row", axis=0, tiled=True)
    got_down, grad_full = lax.optimization_barrier((got_down, grad_full))
    grad_down = own_down + got_down.astype(jnp.float32)
    up_part = lax.dot_general(
        mod_full, grad_full, (((0,), (0,)), ((), ())), preferred_element_type=jnp.float32
    )
    grad_mod_in = slot_scatter_sum(
        lax.dot_general(
            grad_full, up_weight, (((1,), (1,)), ((), ())), preferred_element_type=jnp.float32
        ).astype(jnp.bfloat16),
        "col",
        cols_count,
    )
    own_up, got_up = pair_send(up_part, "dp", 1)
    grad_norm = grad_mod_in * (1.0 + scale)
    sums = ring_sum(
        jnp.stack([jnp.sum(grad_norm, axis=1), jnp.sum(grad_norm * normed, axis=1)], axis=0),
        "row",
        rows_count,
    )
    first = sums[0] / full_width
    second = sums[1] / full_width
    grad_tokens = cot + rstd[:, None] * (grad_norm - first[:, None] - normed * second[:, None])
    own_grad = jnp.stack(
        [jnp.sum(grad_mod_in, axis=0), jnp.sum(grad_mod_in * normed, axis=0), grad_gate], axis=0
    )
    placed = jnp.where(
        (jnp.arange(cols_count, dtype=jnp.int32) == col_index)[:, None, None], own_grad[None], 0.0
    )
    got_up, placed = lax.optimization_barrier((got_up, placed))
    grad_up = own_up + got_up.astype(jnp.float32)
    placed = placed + lax.ppermute(placed, "dp", [(0, 1), (1, 0)])
    grad_mod = ring_sum(placed, "col", cols_count)
    cond_f = cond_part.astype(jnp.float32)
    grad_ada = cond_f[0][None, :, None] * grad_mod[0][:, None, :]
    for v in range(1, cols_count):
        grad_ada = grad_ada + cond_f[v][None, :, None] * grad_mod[v][:, None, :]
    return (grad_tokens.astype(jnp.bfloat16), grad_ada, grad_up, grad_down)


def solution(mesh):
    return jax.shard_map(
        body,
        mesh=mesh,
        in_specs=(
            P(("col", "dp"), "row"),
            P(),
            P(None, "col", "row"),
            P("row", "col"),
            P("col", "row"),
            P(("col", "dp"), "row"),
        ),
        out_specs=(
            P(("col", "dp"), "row"),
            P(None, "col", "row"),
            P("row", ("col", "dp")),
            P(("col", "dp"), "row"),
        ),
        check_vma=False,
    )
```

```python
import math

import jax
import jax.numpy as jnp
from jax import lax
from jax.sharding import PartitionSpec as P

tanh_scale = math.sqrt(2.0 / math.pi)


def gelu_tanh(h):
    return 0.5 * h * (1.0 + jnp.tanh(tanh_scale * (h + 0.044715 * h * h * h)))


def gelu_slope(h):
    inner = jnp.tanh(tanh_scale * (h + 0.044715 * h * h * h))
    return 0.5 * (1.0 + inner) + 0.5 * h * (1.0 - inner * inner) * tanh_scale * (
        1.0 + 3.0 * 0.044715 * h * h
    )


def time_features(timesteps, width):
    half = width // 2
    freqs = jnp.exp(-math.log(10000.0) * jnp.arange(half, dtype=jnp.float32) / half)
    angles = timesteps.astype(jnp.float32)[:, None] * freqs[None, :]
    embed = jnp.concatenate([jnp.cos(angles), jnp.sin(angles)], axis=1)
    return jax.nn.silu(embed).astype(jnp.bfloat16)


def shifted(x, axis, n, s):
    return lax.ppermute(x, axis, [(j, (j + s) % n) for j in range(n)])


def slot_gather(x, axis, n):
    return jnp.concatenate([x] + [shifted(x, axis, n, s) for s in range(1, n)], axis=0)


def slot_scatter_sum(parts, axis, n):
    m = parts.shape[0] // n
    total = parts[0:m].astype(jnp.float32)
    for s in range(1, n):
        total = total + shifted(parts[s * m:(s + 1) * m], axis, n, -s).astype(jnp.float32)
    return total


def swapped(x, axis, n, m):
    return lax.ppermute(x, axis, [(j, j ^ m) for j in range(n)])


def ring_sum(x, axis, n):
    m = 1
    while m < n:
        x = x + swapped(x, axis, n, m)
        m *= 2
    return x


def halving_sum(x, axis, n):
    me = lax.axis_index(axis)
    m = n // 2
    while m >= 1:
        bit = (me // m) % 2
        keep = lax.dynamic_slice_in_dim(x, bit * m, m, 0)
        give = lax.dynamic_slice_in_dim(x, (1 - bit) * m, m, 0)
        x = keep + swapped(give, axis, n, m)
        m //= 2
    return x[0]


def pair_send(part, axis, dim):
    d = lax.axis_index(axis)
    half = part.shape[dim] // 2
    own = lax.dynamic_slice_in_dim(part, d * half, half, dim)
    other = lax.dynamic_slice_in_dim(part, (1 - d) * half, half, dim)
    got = lax.ppermute(other.astype(jnp.bfloat16), axis, [(0, 1), (1, 0)])
    return own, got


def body(tokens, timesteps, ada_weight, up_weight, down_weight, cotangent):
    rows_count = lax.axis_size("row")
    cols_count = lax.axis_size("col")
    col_index = lax.axis_index("col")
    tok_rows, width = tokens.shape
    full_width = width * rows_count
    in_width = ada_weight.shape[1]
    cond = time_features(timesteps, full_width)
    cond_part = lax.dynamic_slice_in_dim(cond, col_index * in_width, in_width, 1)
    mod_terms = jnp.einsum("vi,kio->vko", cond_part, ada_weight, preferred_element_type=jnp.float32)
    own_mod = halving_sum(mod_terms, "col", cols_count)
    shift = own_mod[0]
    scale = own_mod[1]
    gate = own_mod[2]
    x = tokens.astype(jnp.float32)
    stats = ring_sum(jnp.stack([jnp.sum(x, axis=1), jnp.sum(x * x, axis=1)], axis=0), "row", rows_count)
    mean = stats[0] / full_width
    var = stats[1] / full_width - mean * mean
    rstd = lax.rsqrt(var + 1e-06)
    normed = (x - mean[:, None]) * rstd[:, None]
    modulated = (normed * (1.0 + scale) + shift).astype(jnp.bfloat16)
    cot = cotangent.astype(jnp.float32)
    grad_branch = (cot * gate).astype(jnp.bfloat16)
    mod_full = slot_gather(modulated, "col", cols_count)
    branch_full = slot_gather(grad_branch, "col", cols_count)
    hidden_own = lax.psum_scatter(
        jnp.dot(mod_full, up_weight, preferred_element_type=jnp.float32).astype(jnp.bfloat16),
        "row",
        scatter_dimension=0,
        tiled=True,
    ).astype(jnp.float32)
    act_own = gelu_tanh(hidden_own).astype(jnp.bfloat16)
    act_full = lax.all_gather(act_own, "row", axis=0, tiled=True)
    branch = slot_scatter_sum(
        jnp.dot(act_full, down_weight, preferred_element_type=jnp.float32).astype(jnp.bfloat16),
        "col",
        cols_count,
    )
    grad_gate = jnp.sum(cot * branch, axis=0)
    down_part = lax.dot_general(
        act_full, branch_full, (((0,), (0,)), ((), ())), preferred_element_type=jnp.float32
    )
    grad_act = lax.psum_scatter(
        lax.dot_general(
            branch_full, down_weight, (((1,), (1,)), ((), ())), preferred_element_type=jnp.float32
        ).astype(jnp.bfloat16),
        "row",
        scatter_dimension=0,
        tiled=True,
    ).astype(jnp.float32)
    own_down, got_down = pair_send(down_part, "dp", 0)
    grad_hidden = (grad_act * gelu_slope(hidden_own)).astype(jnp.bfloat16)
    grad_full = lax.all_gather(grad_hidden, "row", axis=0, tiled=True)
    got_down, branch, grad_full = lax.optimization_barrier((got_down, branch, grad_full))
    grad_down = own_down + got_down.astype(jnp.float32)
    up_part = lax.dot_general(
        mod_full, grad_full, (((0,), (0,)), ((), ())), preferred_element_type=jnp.float32
    )
    grad_mod_in = slot_scatter_sum(
        lax.dot_general(
            grad_full, up_weight, (((1,), (1,)), ((), ())), preferred_element_type=jnp.float32
        ).astype(jnp.bfloat16),
        "col",
        cols_count,
    )
    grad_norm = grad_mod_in * (1.0 + scale)
    sums = ring_sum(
        jnp.stack([jnp.sum(grad_norm, axis=1), jnp.sum(grad_norm * normed, axis=1)], axis=0),
        "row",
        rows_count,
    )
    first = sums[0] / full_width
    second = sums[1] / full_width
    grad_tokens = cot + rstd[:, None] * (grad_norm - first[:, None] - normed * second[:, None])
    own_grad = jnp.stack(
        [jnp.sum(grad_mod_in, axis=0), jnp.sum(grad_mod_in * normed, axis=0), grad_gate], axis=0
    )
    placed = jnp.where(
        (jnp.arange(cols_count, dtype=jnp.int32) == col_index)[:, None, None], own_grad[None], 0.0
    )
    placed = placed + lax.ppermute(placed, "dp", [(0, 1), (1, 0)])
    grad_mod = ring_sum(placed, "col", cols_count)
    up_part, grad_mod = lax.optimization_barrier((up_part, grad_mod))
    own_up, got_up = pair_send(up_part, "dp", 1)
    grad_up = own_up + got_up.astype(jnp.float32)
    cond_f = cond_part.astype(jnp.float32)
    grad_ada = cond_f[0][None, :, None] * grad_mod[0][:, None, :]
    for v in range(1, cols_count):
        grad_ada = grad_ada + cond_f[v][None, :, None] * grad_mod[v][:, None, :]
    return (grad_tokens.astype(jnp.bfloat16), grad_ada, grad_up, grad_down)


def solution(mesh):
    return jax.shard_map(
        body,
        mesh=mesh,
        in_specs=(
            P(("col", "dp"), "row"),
            P(),
            P(None, "col", "row"),
            P("row", "col"),
            P("col", "row"),
            P(("col", "dp"), "row"),
        ),
        out_specs=(
            P(("col", "dp"), "row"),
            P(None, "col", "row"),
            P("row", ("col", "dp")),
            P(("col", "dp"), "row"),
        ),
        check_vma=False,
    )
```

```python
import math

import jax
import jax.numpy as jnp
from jax import lax
from jax.sharding import PartitionSpec as P

tanh_scale = math.sqrt(2.0 / math.pi)


def gelu_tanh(h):
    return 0.5 * h * (1.0 + jnp.tanh(tanh_scale * (h + 0.044715 * h * h * h)))


def gelu_slope(h):
    inner = jnp.tanh(tanh_scale * (h + 0.044715 * h * h * h))
    return 0.5 * (1.0 + inner) + 0.5 * h * (1.0 - inner * inner) * tanh_scale * (
        1.0 + 3.0 * 0.044715 * h * h
    )


def time_features(timesteps, width):
    half = width // 2
    freqs = jnp.exp(-math.log(10000.0) * jnp.arange(half, dtype=jnp.float32) / half)
    angles = timesteps.astype(jnp.float32)[:, None] * freqs[None, :]
    embed = jnp.concatenate([jnp.cos(angles), jnp.sin(angles)], axis=1)
    return jax.nn.silu(embed).astype(jnp.bfloat16)


def shifted(x, axis, n, s):
    return lax.ppermute(x, axis, [(j, (j + s) % n) for j in range(n)])


def slot_gather(x, axis, n):
    return jnp.concatenate([x] + [shifted(x, axis, n, s) for s in range(1, n)], axis=0)


def slot_scatter_sum(parts, axis, n):
    m = parts.shape[0] // n
    total = parts[0:m].astype(jnp.float32)
    for s in range(1, n):
        total = total + shifted(parts[s * m:(s + 1) * m], axis, n, -s).astype(jnp.float32)
    return total


def swapped(x, axis, n, m):
    return lax.ppermute(x, axis, [(j, j ^ m) for j in range(n)])


def ring_sum(x, axis, n):
    m = 1
    while m < n:
        x = x + swapped(x, axis, n, m)
        m *= 2
    return x


def halving_sum(x, axis, n):
    me = lax.axis_index(axis)
    m = n // 2
    while m >= 1:
        bit = (me // m) % 2
        keep = lax.dynamic_slice_in_dim(x, bit * m, m, 0)
        give = lax.dynamic_slice_in_dim(x, (1 - bit) * m, m, 0)
        x = keep + swapped(give, axis, n, m)
        m //= 2
    return x[0]


def pair_send(part, axis, dim):
    d = lax.axis_index(axis)
    half = part.shape[dim] // 2
    own = lax.dynamic_slice_in_dim(part, d * half, half, dim)
    other = lax.dynamic_slice_in_dim(part, (1 - d) * half, half, dim)
    got = lax.ppermute(other.astype(jnp.bfloat16), axis, [(0, 1), (1, 0)])
    return own, got


def body(tokens, timesteps, ada_weight, up_weight, down_weight, cotangent):
    rows_count = lax.axis_size("row")
    cols_count = lax.axis_size("col")
    col_index = lax.axis_index("col")
    tok_rows, width = tokens.shape
    full_width = width * rows_count
    in_width = ada_weight.shape[1]
    cond = time_features(timesteps, full_width)
    cond_part = lax.dynamic_slice_in_dim(cond, col_index * in_width, in_width, 1)
    mod_terms = jnp.einsum("vi,kio->vko", cond_part, ada_weight, preferred_element_type=jnp.float32)
    own_mod = halving_sum(mod_terms, "col", cols_count)
    shift = own_mod[0]
    scale = own_mod[1]
    gate = own_mod[2]
    x = tokens.astype(jnp.float32)
    stats = ring_sum(jnp.stack([jnp.sum(x, axis=1), jnp.sum(x * x, axis=1)], axis=0), "row", rows_count)
    mean = stats[0] / full_width
    var = stats[1] / full_width - mean * mean
    rstd = lax.rsqrt(var + 1e-06)
    normed = (x - mean[:, None]) * rstd[:, None]
    modulated = (normed * (1.0 + scale) + shift).astype(jnp.bfloat16)
    cot = cotangent.astype(jnp.float32)
    grad_branch = (cot * gate).astype(jnp.bfloat16)
    mod_full = slot_gather(modulated, "col", cols_count)
    branch_full = slot_gather(grad_branch, "col", cols_count)
    hidden_own = lax.psum_scatter(
        jnp.dot(mod_full, up_weight, preferred_element_type=jnp.float32).astype(jnp.bfloat16),
        "row",
        scatter_dimension=0,
        tiled=True,
    ).astype(jnp.float32)
    act_own = gelu_tanh(hidden_own).astype(jnp.bfloat16)
    cot_src, act_own = lax.optimization_barrier((cotangent, act_own))
    cot_full = slot_gather(cot_src, "col", cols_count)
    act_full = lax.all_gather(act_own, "row", axis=0, tiled=True)
    cot_full, act_full = lax.optimization_barrier((cot_full, act_full))
    branch_part = jnp.dot(act_full, down_weight, preferred_element_type=jnp.float32).astype(jnp.bfloat16)
    gate_terms = cot_full.astype(jnp.float32) * branch_part.astype(jnp.float32)
    gate_slots = jnp.sum(gate_terms.reshape((cols_count, tok_rows) + gate_terms.shape[1:]), axis=1)
    slot_vol = (col_index - jnp.arange(cols_count, dtype=jnp.int32)) % cols_count
    gate_by_vol = jnp.take(gate_slots, slot_vol, axis=0)
    down_part = lax.dot_general(
        act_full, branch_full, (((0,), (0,)), ((), ())), preferred_element_type=jnp.float32
    )
    grad_act = lax.psum_scatter(
        lax.dot_general(
            branch_full, down_weight, (((1,), (1,)), ((), ())), preferred_element_type=jnp.float32
        ).astype(jnp.bfloat16),
        "row",
        scatter_dimension=0,
        tiled=True,
    ).astype(jnp.float32)
    own_down, got_down = pair_send(down_part, "dp", 0)
    grad_hidden = (grad_act * gelu_slope(hidden_own)).astype(jnp.bfloat16)
    grad_full = lax.all_gather(grad_hidden, "row", axis=0, tiled=True)
    got_down, grad_full = lax.optimization_barrier((got_down, grad_full))
    grad_down = own_down + got_down.astype(jnp.float32)
    up_part = lax.dot_general(
        mod_full, grad_full, (((0,), (0,)), ((), ())), preferred_element_type=jnp.float32
    )
    grad_mod_in = slot_scatter_sum(
        lax.dot_general(
            grad_full, up_weight, (((1,), (1,)), ((), ())), preferred_element_type=jnp.float32
        ).astype(jnp.bfloat16),
        "col",
        cols_count,
    )
    grad_norm = grad_mod_in * (1.0 + scale)
    sums = ring_sum(
        jnp.stack([jnp.sum(grad_norm, axis=1), jnp.sum(grad_norm * normed, axis=1)], axis=0),
        "row",
        rows_count,
    )
    first = sums[0] / full_width
    second = sums[1] / full_width
    grad_tokens = cot + rstd[:, None] * (grad_norm - first[:, None] - normed * second[:, None])
    own_grad = jnp.stack([jnp.sum(grad_mod_in, axis=0), jnp.sum(grad_mod_in * normed, axis=0)], axis=0)
    placed = jnp.where(
        (jnp.arange(cols_count, dtype=jnp.int32) == col_index)[:, None, None], own_grad[None], 0.0
    )
    placed = jnp.concatenate([placed, gate_by_vol[:, None, :]], axis=1)
    placed = placed + lax.ppermute(placed, "dp", [(0, 1), (1, 0)])
    grad_mod = ring_sum(placed, "col", cols_count)
    up_part, grad_mod = lax.optimization_barrier((up_part, grad_mod))
    own_up, got_up = pair_send(up_part, "dp", 1)
    grad_up = own_up + got_up.astype(jnp.float32)
    cond_f = cond_part.astype(jnp.float32)
    grad_ada = cond_f[0][None, :, None] * grad_mod[0][:, None, :]
    for v in range(1, cols_count):
        grad_ada = grad_ada + cond_f[v][None, :, None] * grad_mod[v][:, None, :]
    return (grad_tokens.astype(jnp.bfloat16), grad_ada, grad_up, grad_down)


def solution(mesh):
    return jax.shard_map(
        body,
        mesh=mesh,
        in_specs=(
            P(("col", "dp"), "row"),
            P(),
            P(None, "col", "row"),
            P("row", "col"),
            P("col", "row"),
            P(("col", "dp"), "row"),
        ),
        out_specs=(
            P(("col", "dp"), "row"),
            P(None, "col", "row"),
            P("row", ("col", "dp")),
            P(("col", "dp"), "row"),
        ),
        check_vma=False,
    )
```

```python
import math

import jax
import jax.numpy as jnp
from jax import lax
from jax.sharding import PartitionSpec as P

tanh_scale = math.sqrt(2.0 / math.pi)


def gelu_tanh(h):
    return 0.5 * h * (1.0 + jnp.tanh(tanh_scale * (h + 0.044715 * h * h * h)))


def gelu_slope(h):
    inner = jnp.tanh(tanh_scale * (h + 0.044715 * h * h * h))
    return 0.5 * (1.0 + inner) + 0.5 * h * (1.0 - inner * inner) * tanh_scale * (
        1.0 + 3.0 * 0.044715 * h * h
    )


def time_features(timesteps, width):
    half = width // 2
    freqs = jnp.exp(-math.log(10000.0) * jnp.arange(half, dtype=jnp.float32) / half)
    angles = timesteps.astype(jnp.float32)[:, None] * freqs[None, :]
    embed = jnp.concatenate([jnp.cos(angles), jnp.sin(angles)], axis=1)
    return jax.nn.silu(embed).astype(jnp.bfloat16)


def shifted(x, axis, n, s):
    return lax.ppermute(x, axis, [(j, (j + s) % n) for j in range(n)])


def slot_gather(x, axis, n):
    return jnp.concatenate([x] + [shifted(x, axis, n, s) for s in range(1, n)], axis=0)


def slot_scatter_sum(parts, axis, n):
    m = parts.shape[0] // n
    total = parts[0:m].astype(jnp.float32)
    for s in range(1, n):
        total = total + shifted(parts[s * m:(s + 1) * m], axis, n, -s).astype(jnp.float32)
    return total


def swapped(x, axis, n, m):
    return lax.ppermute(x, axis, [(j, j ^ m) for j in range(n)])


def ring_sum(x, axis, n):
    m = 1
    while m < n:
        x = x + swapped(x, axis, n, m)
        m *= 2
    return x


def xor_steps(x, axis, n, masks):
    for m in masks:
        x = x + swapped(x, axis, n, m)
    return x


def halving_sum(x, axis, n):
    me = lax.axis_index(axis)
    m = n // 2
    while m >= 1:
        bit = (me // m) % 2
        keep = lax.dynamic_slice_in_dim(x, bit * m, m, 0)
        give = lax.dynamic_slice_in_dim(x, (1 - bit) * m, m, 0)
        x = keep + swapped(give, axis, n, m)
        m //= 2
    return x[0]


def pair_send(part, axis, dim):
    d = lax.axis_index(axis)
    half = part.shape[dim] // 2
    own = lax.dynamic_slice_in_dim(part, d * half, half, dim)
    other = lax.dynamic_slice_in_dim(part, (1 - d) * half, half, dim)
    got = lax.ppermute(other.astype(jnp.bfloat16), axis, [(0, 1), (1, 0)])
    return own, got


def body(tokens, timesteps, ada_weight, up_weight, down_weight, cotangent):
    rows_count = lax.axis_size("row")
    cols_count = lax.axis_size("col")
    col_index = lax.axis_index("col")
    tok_rows, width = tokens.shape
    full_width = width * rows_count
    in_width = ada_weight.shape[1]
    cond = time_features(timesteps, full_width)
    cond_part = lax.dynamic_slice_in_dim(cond, col_index * in_width, in_width, 1)
    mod_terms = jnp.einsum("vi,kio->vko", cond_part, ada_weight, preferred_element_type=jnp.float32)
    own_mod = halving_sum(mod_terms, "col", cols_count)
    shift = own_mod[0]
    scale = own_mod[1]
    gate = own_mod[2]
    x = tokens.astype(jnp.float32)
    stats = ring_sum(jnp.stack([jnp.sum(x, axis=1), jnp.sum(x * x, axis=1)], axis=0), "row", rows_count)
    mean = stats[0] / full_width
    var = stats[1] / full_width - mean * mean
    rstd = lax.rsqrt(var + 1e-06)
    normed = (x - mean[:, None]) * rstd[:, None]
    modulated = (normed * (1.0 + scale) + shift).astype(jnp.bfloat16)
    cot = cotangent.astype(jnp.float32)
    grad_branch = (cot * gate).astype(jnp.bfloat16)
    mod_full = slot_gather(modulated, "col", cols_count)
    branch_full = slot_gather(grad_branch, "col", cols_count)
    hidden_own = lax.psum_scatter(
        jnp.dot(mod_full, up_weight, preferred_element_type=jnp.float32).astype(jnp.bfloat16),
        "row",
        scatter_dimension=0,
        tiled=True,
    ).astype(jnp.float32)
    act_own = gelu_tanh(hidden_own).astype(jnp.bfloat16)
    cot_src, act_own = lax.optimization_barrier((cotangent, act_own))
    cot_full = slot_gather(cot_src, "col", cols_count)
    act_full = lax.all_gather(act_own, "row", axis=0, tiled=True)
    cot_full, act_full = lax.optimization_barrier((cot_full, act_full))
    branch_part = jnp.dot(act_full, down_weight, preferred_element_type=jnp.float32).astype(jnp.bfloat16)
    gate_terms = cot_full.astype(jnp.float32) * branch_part.astype(jnp.float32)
    gate_slots = jnp.sum(gate_terms.reshape((cols_count, tok_rows) + gate_terms.shape[1:]), axis=1)
    slot_vol = (col_index - jnp.arange(cols_count, dtype=jnp.int32)) % cols_count
    gate_by_vol = jnp.take(gate_slots, slot_vol, axis=0)
    down_part = lax.dot_general(
        act_full, branch_full, (((0,), (0,)), ((), ())), preferred_element_type=jnp.float32
    )
    grad_act = lax.psum_scatter(
        lax.dot_general(
            branch_full, down_weight, (((1,), (1,)), ((), ())), preferred_element_type=jnp.float32
        ).astype(jnp.bfloat16),
        "row",
        scatter_dimension=0,
        tiled=True,
    ).astype(jnp.float32)
    own_down, got_down = pair_send(down_part, "dp", 0)
    grad_hidden = (grad_act * gelu_slope(hidden_own)).astype(jnp.bfloat16)
    grad_full = lax.all_gather(grad_hidden, "row", axis=0, tiled=True)
    got_down, grad_full = lax.optimization_barrier((got_down, grad_full))
    grad_down = own_down + got_down.astype(jnp.float32)
    up_part = lax.dot_general(
        mod_full, grad_full, (((0,), (0,)), ((), ())), preferred_element_type=jnp.float32
    )
    grad_mod_in = slot_scatter_sum(
        lax.dot_general(
            grad_full, up_weight, (((1,), (1,)), ((), ())), preferred_element_type=jnp.float32
        ).astype(jnp.bfloat16),
        "col",
        cols_count,
    )
    grad_norm = grad_mod_in * (1.0 + scale)
    sums = ring_sum(
        jnp.stack([jnp.sum(grad_norm, axis=1), jnp.sum(grad_norm * normed, axis=1)], axis=0),
        "row",
        rows_count,
    )
    first = sums[0] / full_width
    second = sums[1] / full_width
    grad_tokens = cot + rstd[:, None] * (grad_norm - first[:, None] - normed * second[:, None])
    own_grad = jnp.stack([jnp.sum(grad_mod_in, axis=0), jnp.sum(grad_mod_in * normed, axis=0)], axis=0)
    placed = jnp.where(
        (jnp.arange(cols_count, dtype=jnp.int32) == col_index)[:, None, None], own_grad[None], 0.0
    )
    placed = jnp.concatenate([placed, gate_by_vol[:, None, :]], axis=1)
    placed = placed + lax.ppermute(placed, "dp", [(0, 1), (1, 0)])
    far = cols_count // 2
    placed = xor_steps(placed, "col", cols_count, [far])
    up_part, placed = lax.optimization_barrier((up_part, placed))
    near = []
    m = 1
    while m < far:
        near.append(m)
        m *= 2
    grad_mod = xor_steps(placed, "col", cols_count, near)
    own_up, got_up = pair_send(up_part, "dp", 1)
    grad_up = own_up + got_up.astype(jnp.float32)
    cond_f = cond_part.astype(jnp.float32)
    grad_ada = cond_f[0][None, :, None] * grad_mod[0][:, None, :]
    for v in range(1, cols_count):
        grad_ada = grad_ada + cond_f[v][None, :, None] * grad_mod[v][:, None, :]
    return (grad_tokens.astype(jnp.bfloat16), grad_ada, grad_up, grad_down)


def solution(mesh):
    return jax.shard_map(
        body,
        mesh=mesh,
        in_specs=(
            P(("col", "dp"), "row"),
            P(),
            P(None, "col", "row"),
            P("row", "col"),
            P("col", "row"),
            P(("col", "dp"), "row"),
        ),
        out_specs=(
            P(("col", "dp"), "row"),
            P(None, "col", "row"),
            P("row", ("col", "dp")),
            P(("col", "dp"), "row"),
        ),
        check_vma=False,
    )
```

```python
import math

import jax
import jax.numpy as jnp
from jax import lax
from jax.sharding import PartitionSpec as P

tanh_scale = math.sqrt(2.0 / math.pi)


def gelu_tanh(h):
    return 0.5 * h * (1.0 + jnp.tanh(tanh_scale * (h + 0.044715 * h * h * h)))


def gelu_slope(h):
    inner = jnp.tanh(tanh_scale * (h + 0.044715 * h * h * h))
    return 0.5 * (1.0 + inner) + 0.5 * h * (1.0 - inner * inner) * tanh_scale * (
        1.0 + 3.0 * 0.044715 * h * h
    )


def time_features(timesteps, width):
    half = width // 2
    freqs = jnp.exp(-math.log(10000.0) * jnp.arange(half, dtype=jnp.float32) / half)
    angles = timesteps.astype(jnp.float32)[:, None] * freqs[None, :]
    embed = jnp.concatenate([jnp.cos(angles), jnp.sin(angles)], axis=1)
    return jax.nn.silu(embed).astype(jnp.bfloat16)


def shifted(x, axis, n, s):
    return lax.ppermute(x, axis, [(j, (j + s) % n) for j in range(n)])


def slot_gather(x, axis, n):
    return jnp.concatenate([x] + [shifted(x, axis, n, s) for s in range(1, n)], axis=0)


def slot_scatter_sum(parts, axis, n):
    m = parts.shape[0] // n
    total = parts[0:m].astype(jnp.float32)
    for s in range(1, n):
        total = total + shifted(parts[s * m:(s + 1) * m], axis, n, -s).astype(jnp.float32)
    return total


def swapped(x, axis, n, m):
    return lax.ppermute(x, axis, [(j, j ^ m) for j in range(n)])


def ring_sum(x, axis, n):
    m = 1
    while m < n:
        x = x + swapped(x, axis, n, m)
        m *= 2
    return x


def xor_steps(x, axis, n, masks):
    for m in masks:
        x = x + swapped(x, axis, n, m)
    return x


def halving_sum(x, axis, n):
    me = lax.axis_index(axis)
    m = n // 2
    while m >= 1:
        bit = (me // m) % 2
        keep = lax.dynamic_slice_in_dim(x, bit * m, m, 0)
        give = lax.dynamic_slice_in_dim(x, (1 - bit) * m, m, 0)
        x = keep + swapped(give, axis, n, m)
        m //= 2
    return x[0]


def pair_send(part, axis, dim):
    d = lax.axis_index(axis)
    half = part.shape[dim] // 2
    own = lax.dynamic_slice_in_dim(part, d * half, half, dim)
    other = lax.dynamic_slice_in_dim(part, (1 - d) * half, half, dim)
    got = lax.ppermute(other.astype(jnp.bfloat16), axis, [(0, 1), (1, 0)])
    return own, got


def body(tokens, timesteps, ada_weight, up_weight, down_weight, cotangent):
    rows_count = lax.axis_size("row")
    cols_count = lax.axis_size("col")
    col_index = lax.axis_index("col")
    tok_rows, width = tokens.shape
    full_width = width * rows_count
    in_width = ada_weight.shape[1]
    cond = time_features(timesteps, full_width)
    cond_part = lax.dynamic_slice_in_dim(cond, col_index * in_width, in_width, 1)
    mod_terms = jnp.einsum("vi,kio->vko", cond_part, ada_weight, preferred_element_type=jnp.float32)
    mod_all = ring_sum(mod_terms, "col", cols_count)
    own_mod = lax.dynamic_index_in_dim(mod_all, col_index, 0, keepdims=False)
    cot_full = slot_gather(cotangent, "col", cols_count)
    slot_vol = (col_index - jnp.arange(cols_count, dtype=jnp.int32)) % cols_count
    shift = own_mod[0]
    scale = own_mod[1]
    x = tokens.astype(jnp.float32)
    stats = ring_sum(jnp.stack([jnp.sum(x, axis=1), jnp.sum(x * x, axis=1)], axis=0), "row", rows_count)
    mean = stats[0] / full_width
    var = stats[1] / full_width - mean * mean
    rstd = lax.rsqrt(var + 1e-06)
    normed = (x - mean[:, None]) * rstd[:, None]
    modulated = (normed * (1.0 + scale) + shift).astype(jnp.bfloat16)
    cot = cotangent.astype(jnp.float32)
    gate_slots = jnp.take(mod_all[:, 2], slot_vol, axis=0)
    cot_slots = cot_full.astype(jnp.float32).reshape((cols_count, tok_rows, width))
    branch_full = (cot_slots * gate_slots[:, None, :]).astype(jnp.bfloat16).reshape(cot_full.shape)
    mod_full = slot_gather(modulated, "col", cols_count)
    hidden_own = lax.psum_scatter(
        jnp.dot(mod_full, up_weight, preferred_element_type=jnp.float32).astype(jnp.bfloat16),
        "row",
        scatter_dimension=0,
        tiled=True,
    ).astype(jnp.float32)
    act_own = gelu_tanh(hidden_own).astype(jnp.bfloat16)
    act_full = lax.all_gather(act_own, "row", axis=0, tiled=True)
    branch_part = jnp.dot(act_full, down_weight, preferred_element_type=jnp.float32).astype(jnp.bfloat16)
    gate_terms = cot_full.astype(jnp.float32) * branch_part.astype(jnp.float32)
    gate_sums = jnp.sum(gate_terms.reshape((cols_count, tok_rows) + gate_terms.shape[1:]), axis=1)
    gate_by_vol = jnp.take(gate_sums, slot_vol, axis=0)
    down_part = lax.dot_general(
        act_full, branch_full, (((0,), (0,)), ((), ())), preferred_element_type=jnp.float32
    )
    grad_act = lax.psum_scatter(
        lax.dot_general(
            branch_full, down_weight, (((1,), (1,)), ((), ())), preferred_element_type=jnp.float32
        ).astype(jnp.bfloat16),
        "row",
        scatter_dimension=0,
        tiled=True,
    ).astype(jnp.float32)
    own_down, got_down = pair_send(down_part, "dp", 0)
    grad_hidden = (grad_act * gelu_slope(hidden_own)).astype(jnp.bfloat16)
    grad_full = lax.all_gather(grad_hidden, "row", axis=0, tiled=True)
    got_down, grad_full = lax.optimization_barrier((got_down, grad_full))
    grad_down = own_down + got_down.astype(jnp.float32)
    up_part = lax.dot_general(
        mod_full, grad_full, (((0,), (0,)), ((), ())), preferred_element_type=jnp.float32
    )
    grad_mod_in = slot_scatter_sum(
        lax.dot_general(
            grad_full, up_weight, (((1,), (1,)), ((), ())), preferred_element_type=jnp.float32
        ).astype(jnp.bfloat16),
        "col",
        cols_count,
    )
    grad_norm = grad_mod_in * (1.0 + scale)
    sums = ring_sum(
        jnp.stack([jnp.sum(grad_norm, axis=1), jnp.sum(grad_norm * normed, axis=1)], axis=0),
        "row",
        rows_count,
    )
    first = sums[0] / full_width
    second = sums[1] / full_width
    grad_tokens = cot + rstd[:, None] * (grad_norm - first[:, None] - normed * second[:, None])
    own_grad = jnp.stack([jnp.sum(grad_mod_in, axis=0), jnp.sum(grad_mod_in * normed, axis=0)], axis=0)
    placed = jnp.where(
        (jnp.arange(cols_count, dtype=jnp.int32) == col_index)[:, None, None], own_grad[None], 0.0
    )
    placed = jnp.concatenate([placed, gate_by_vol[:, None, :]], axis=1)
    placed = placed + lax.ppermute(placed, "dp", [(0, 1), (1, 0)])
    far = cols_count // 2
    placed = xor_steps(placed, "col", cols_count, [far])
    up_part, placed = lax.optimization_barrier((up_part, placed))
    near = []
    m = 1
    while m < far:
        near.append(m)
        m *= 2
    grad_mod = xor_steps(placed, "col", cols_count, near)
    own_up, got_up = pair_send(up_part, "dp", 1)
    grad_up = own_up + got_up.astype(jnp.float32)
    cond_f = cond_part.astype(jnp.float32)
    grad_ada = cond_f[0][None, :, None] * grad_mod[0][:, None, :]
    for v in range(1, cols_count):
        grad_ada = grad_ada + cond_f[v][None, :, None] * grad_mod[v][:, None, :]
    return (grad_tokens.astype(jnp.bfloat16), grad_ada, grad_up, grad_down)


def solution(mesh):
    return jax.shard_map(
        body,
        mesh=mesh,
        in_specs=(
            P(("col", "dp"), "row"),
            P(),
            P(None, "col", "row"),
            P("row", "col"),
            P("col", "row"),
            P(("col", "dp"), "row"),
        ),
        out_specs=(
            P(("col", "dp"), "row"),
            P(None, "col", "row"),
            P("row", ("col", "dp")),
            P(("col", "dp"), "row"),
        ),
        check_vma=False,
    )
```

```python
import math

import jax
import jax.numpy as jnp
from jax import lax
from jax.sharding import PartitionSpec as P

tanh_scale = math.sqrt(2.0 / math.pi)


def gelu_tanh(h):
    return 0.5 * h * (1.0 + jnp.tanh(tanh_scale * (h + 0.044715 * h * h * h)))


def gelu_slope(h):
    inner = jnp.tanh(tanh_scale * (h + 0.044715 * h * h * h))
    return 0.5 * (1.0 + inner) + 0.5 * h * (1.0 - inner * inner) * tanh_scale * (
        1.0 + 3.0 * 0.044715 * h * h
    )


def time_features(timesteps, width):
    half = width // 2
    freqs = jnp.exp(-math.log(10000.0) * jnp.arange(half, dtype=jnp.float32) / half)
    angles = timesteps.astype(jnp.float32)[:, None] * freqs[None, :]
    embed = jnp.concatenate([jnp.cos(angles), jnp.sin(angles)], axis=1)
    return jax.nn.silu(embed).astype(jnp.bfloat16)


def shifted(x, axis, n, s):
    return lax.ppermute(x, axis, [(j, (j + s) % n) for j in range(n)])


def slot_gather(x, axis, n):
    return jnp.concatenate([x] + [shifted(x, axis, n, s) for s in range(1, n)], axis=0)


def slot_scatter_sum(parts, axis, n):
    m = parts.shape[0] // n
    total = parts[0:m].astype(jnp.float32)
    for s in range(1, n):
        total = total + shifted(parts[s * m:(s + 1) * m], axis, n, -s).astype(jnp.float32)
    return total


def swapped(x, axis, n, m):
    return lax.ppermute(x, axis, [(j, j ^ m) for j in range(n)])


def ring_sum(x, axis, n):
    m = 1
    while m < n:
        x = x + swapped(x, axis, n, m)
        m *= 2
    return x


def xor_steps(x, axis, n, masks):
    for m in masks:
        x = x + swapped(x, axis, n, m)
    return x


def halving_sum(x, axis, n):
    me = lax.axis_index(axis)
    m = n // 2
    while m >= 1:
        bit = (me // m) % 2
        keep = lax.dynamic_slice_in_dim(x, bit * m, m, 0)
        give = lax.dynamic_slice_in_dim(x, (1 - bit) * m, m, 0)
        x = keep + swapped(give, axis, n, m)
        m //= 2
    return x[0]


def pair_send(part, axis, dim):
    d = lax.axis_index(axis)
    half = part.shape[dim] // 2
    own = lax.dynamic_slice_in_dim(part, d * half, half, dim)
    other = lax.dynamic_slice_in_dim(part, (1 - d) * half, half, dim)
    got = lax.ppermute(other.astype(jnp.bfloat16), axis, [(0, 1), (1, 0)])
    return own, got


def body(tokens, timesteps, ada_weight, up_weight, down_weight, cotangent):
    rows_count = lax.axis_size("row")
    cols_count = lax.axis_size("col")
    col_index = lax.axis_index("col")
    tok_rows, width = tokens.shape
    full_width = width * rows_count
    in_width = ada_weight.shape[1]
    cond = time_features(timesteps, full_width)
    cond_part = lax.dynamic_slice_in_dim(cond, col_index * in_width, in_width, 1)
    mod_terms = jnp.einsum("vi,kio->vko", cond_part, ada_weight, preferred_element_type=jnp.float32)
    mod_all = ring_sum(mod_terms, "col", cols_count)
    own_mod = lax.dynamic_index_in_dim(mod_all, col_index, 0, keepdims=False)
    cot_full = slot_gather(cotangent, "col", cols_count)
    slot_vol = (col_index - jnp.arange(cols_count, dtype=jnp.int32)) % cols_count
    shift = own_mod[0]
    scale = own_mod[1]
    x = tokens.astype(jnp.float32)
    stats = ring_sum(jnp.stack([jnp.sum(x, axis=1), jnp.sum(x * x, axis=1)], axis=0), "row", rows_count)
    mean = stats[0] / full_width
    var = stats[1] / full_width - mean * mean
    rstd = lax.rsqrt(var + 1e-06)
    normed = (x - mean[:, None]) * rstd[:, None]
    modulated = (normed * (1.0 + scale) + shift).astype(jnp.bfloat16)
    cot = cotangent.astype(jnp.float32)
    gate_slots = jnp.take(mod_all[:, 2], slot_vol, axis=0)
    cot_slots = cot_full.astype(jnp.float32).reshape((cols_count, tok_rows, width))
    branch_full = (cot_slots * gate_slots[:, None, :]).astype(jnp.bfloat16).reshape(cot_full.shape)
    mod_full = slot_gather(modulated, "col", cols_count)
    hidden_own = lax.psum_scatter(
        jnp.dot(mod_full, up_weight, preferred_element_type=jnp.float32).astype(jnp.bfloat16),
        "row",
        scatter_dimension=0,
        tiled=True,
    ).astype(jnp.float32)
    act_own = gelu_tanh(hidden_own).astype(jnp.bfloat16)
    act_full = lax.all_gather(act_own, "row", axis=0, tiled=True)
    branch_part = jnp.dot(act_full, down_weight, preferred_element_type=jnp.float32).astype(jnp.bfloat16)
    gate_terms = cot_full.astype(jnp.float32) * branch_part.astype(jnp.float32)
    gate_sums = jnp.sum(gate_terms.reshape((cols_count, tok_rows) + gate_terms.shape[1:]), axis=1)
    gate_by_vol = jnp.take(gate_sums, slot_vol, axis=0)
    down_part = lax.dot_general(
        act_full, branch_full, (((0,), (0,)), ((), ())), preferred_element_type=jnp.float32
    )
    grad_act = lax.psum_scatter(
        lax.dot_general(
            branch_full, down_weight, (((1,), (1,)), ((), ())), preferred_element_type=jnp.float32
        ).astype(jnp.bfloat16),
        "row",
        scatter_dimension=0,
        tiled=True,
    ).astype(jnp.float32)
    own_down, got_down = pair_send(down_part, "dp", 0)
    grad_hidden = (grad_act * gelu_slope(hidden_own)).astype(jnp.bfloat16)
    grad_full = lax.all_gather(grad_hidden, "row", axis=0, tiled=True)
    grad_down = own_down + got_down.astype(jnp.float32)
    grad_down, grad_full = lax.optimization_barrier((grad_down, grad_full))
    up_part = lax.dot_general(
        mod_full, grad_full, (((0,), (0,)), ((), ())), preferred_element_type=jnp.float32
    )
    grad_mod_in = slot_scatter_sum(
        lax.dot_general(
            grad_full, up_weight, (((1,), (1,)), ((), ())), preferred_element_type=jnp.float32
        ).astype(jnp.bfloat16),
        "col",
        cols_count,
    )
    grad_norm = grad_mod_in * (1.0 + scale)
    sums = ring_sum(
        jnp.stack([jnp.sum(grad_norm, axis=1), jnp.sum(grad_norm * normed, axis=1)], axis=0),
        "row",
        rows_count,
    )
    first = sums[0] / full_width
    second = sums[1] / full_width
    grad_tokens = cot + rstd[:, None] * (grad_norm - first[:, None] - normed * second[:, None])
    own_grad = jnp.stack([jnp.sum(grad_mod_in, axis=0), jnp.sum(grad_mod_in * normed, axis=0)], axis=0)
    placed = jnp.where(
        (jnp.arange(cols_count, dtype=jnp.int32) == col_index)[:, None, None], own_grad[None], 0.0
    )
    placed = jnp.concatenate([placed, gate_by_vol[:, None, :]], axis=1)
    placed = placed + lax.ppermute(placed, "dp", [(0, 1), (1, 0)])
    far = cols_count // 2
    placed = xor_steps(placed, "col", cols_count, [far])
    up_part, placed = lax.optimization_barrier((up_part, placed))
    near = []
    m = 1
    while m < far:
        near.append(m)
        m *= 2
    grad_mod = xor_steps(placed, "col", cols_count, near)
    own_up, got_up = pair_send(up_part, "dp", 1)
    grad_up = own_up + got_up.astype(jnp.float32)
    cond_f = cond_part.astype(jnp.float32)
    grad_ada = cond_f[0][None, :, None] * grad_mod[0][:, None, :]
    for v in range(1, cols_count):
        grad_ada = grad_ada + cond_f[v][None, :, None] * grad_mod[v][:, None, :]
    return (grad_tokens.astype(jnp.bfloat16), grad_ada, grad_up, grad_down)


def solution(mesh):
    return jax.shard_map(
        body,
        mesh=mesh,
        in_specs=(
            P(("col", "dp"), "row"),
            P(),
            P(None, "col", "row"),
            P("row", "col"),
            P("col", "row"),
            P(("col", "dp"), "row"),
        ),
        out_specs=(
            P(("col", "dp"), "row"),
            P(None, "col", "row"),
            P("row", ("col", "dp")),
            P(("col", "dp"), "row"),
        ),
        check_vma=False,
    )
```

```python
import math

import jax
import jax.numpy as jnp
from jax import lax
from jax.sharding import PartitionSpec as P

tanh_scale = math.sqrt(2.0 / math.pi)


def gelu_tanh(h):
    return 0.5 * h * (1.0 + jnp.tanh(tanh_scale * (h + 0.044715 * h * h * h)))


def gelu_slope(h):
    inner = jnp.tanh(tanh_scale * (h + 0.044715 * h * h * h))
    return 0.5 * (1.0 + inner) + 0.5 * h * (1.0 - inner * inner) * tanh_scale * (
        1.0 + 3.0 * 0.044715 * h * h
    )


def time_features(timesteps, width):
    half = width // 2
    freqs = jnp.exp(-math.log(10000.0) * jnp.arange(half, dtype=jnp.float32) / half)
    angles = timesteps.astype(jnp.float32)[:, None] * freqs[None, :]
    embed = jnp.concatenate([jnp.cos(angles), jnp.sin(angles)], axis=1)
    return jax.nn.silu(embed).astype(jnp.bfloat16)


def shifted(x, axis, n, s):
    return lax.ppermute(x, axis, [(j, (j + s) % n) for j in range(n)])


def slot_gather(x, axis, n):
    return jnp.concatenate([x] + [shifted(x, axis, n, s) for s in range(1, n)], axis=0)


def slot_scatter_sum(parts, axis, n):
    m = parts.shape[0] // n
    total = parts[0:m].astype(jnp.float32)
    for s in range(1, n):
        total = total + shifted(parts[s * m:(s + 1) * m], axis, n, -s).astype(jnp.float32)
    return total


def direct_scatter_sum(parts, axis, n):
    me = lax.axis_index(axis)
    m = parts.shape[0] // n
    total = lax.dynamic_slice_in_dim(parts, me * m, m, 0).astype(jnp.float32)
    for s in range(1, n):
        block = lax.dynamic_slice_in_dim(parts, ((me + s) % n) * m, m, 0)
        total = total + shifted(block, axis, n, s).astype(jnp.float32)
    return total


def swapped(x, axis, n, m):
    return lax.ppermute(x, axis, [(j, j ^ m) for j in range(n)])


def ring_sum(x, axis, n):
    m = 1
    while m < n:
        x = x + swapped(x, axis, n, m)
        m *= 2
    return x


def xor_steps(x, axis, n, masks):
    for m in masks:
        x = x + swapped(x, axis, n, m)
    return x


def halving_sum(x, axis, n):
    me = lax.axis_index(axis)
    m = n // 2
    while m >= 1:
        bit = (me // m) % 2
        keep = lax.dynamic_slice_in_dim(x, bit * m, m, 0)
        give = lax.dynamic_slice_in_dim(x, (1 - bit) * m, m, 0)
        x = keep + swapped(give, axis, n, m)
        m //= 2
    return x[0]


def pair_send(part, axis, dim):
    d = lax.axis_index(axis)
    half = part.shape[dim] // 2
    own = lax.dynamic_slice_in_dim(part, d * half, half, dim)
    other = lax.dynamic_slice_in_dim(part, (1 - d) * half, half, dim)
    got = lax.ppermute(other.astype(jnp.bfloat16), axis, [(0, 1), (1, 0)])
    return own, got


def body(tokens, timesteps, ada_weight, up_weight, down_weight, cotangent):
    rows_count = lax.axis_size("row")
    cols_count = lax.axis_size("col")
    col_index = lax.axis_index("col")
    tok_rows, width = tokens.shape
    full_width = width * rows_count
    in_width = ada_weight.shape[1]
    cond = time_features(timesteps, full_width)
    cond_part = lax.dynamic_slice_in_dim(cond, col_index * in_width, in_width, 1)
    mod_terms = jnp.einsum("vi,kio->vko", cond_part, ada_weight, preferred_element_type=jnp.float32)
    mod_all = ring_sum(mod_terms, "col", cols_count)
    own_mod = lax.dynamic_index_in_dim(mod_all, col_index, 0, keepdims=False)
    cot_full = slot_gather(cotangent, "col", cols_count)
    slot_vol = (col_index - jnp.arange(cols_count, dtype=jnp.int32)) % cols_count
    shift = own_mod[0]
    scale = own_mod[1]
    x = tokens.astype(jnp.float32)
    stats = ring_sum(jnp.stack([jnp.sum(x, axis=1), jnp.sum(x * x, axis=1)], axis=0), "row", rows_count)
    mean = stats[0] / full_width
    var = stats[1] / full_width - mean * mean
    rstd = lax.rsqrt(var + 1e-06)
    normed = (x - mean[:, None]) * rstd[:, None]
    modulated = (normed * (1.0 + scale) + shift).astype(jnp.bfloat16)
    cot = cotangent.astype(jnp.float32)
    gate_slots = jnp.take(mod_all[:, 2], slot_vol, axis=0)
    cot_slots = cot_full.astype(jnp.float32).reshape((cols_count, tok_rows, width))
    branch_full = (cot_slots * gate_slots[:, None, :]).astype(jnp.bfloat16).reshape(cot_full.shape)
    mod_full = slot_gather(modulated, "col", cols_count)
    hidden_part = jnp.dot(mod_full, up_weight, preferred_element_type=jnp.float32).astype(jnp.bfloat16)
    split = hidden_part.shape[1] // 2
    hidden_a = lax.psum_scatter(hidden_part[:, :split], "row", scatter_dimension=0, tiled=True)
    hidden_b = direct_scatter_sum(hidden_part[:, split:], "row", rows_count)
    hidden_own = jnp.concatenate([hidden_a.astype(jnp.float32), hidden_b], axis=1)
    act_own = gelu_tanh(hidden_own).astype(jnp.bfloat16)
    act_full = lax.all_gather(act_own, "row", axis=0, tiled=True)
    branch_part = jnp.dot(act_full, down_weight, preferred_element_type=jnp.float32).astype(jnp.bfloat16)
    gate_terms = cot_full.astype(jnp.float32) * branch_part.astype(jnp.float32)
    gate_sums = jnp.sum(gate_terms.reshape((cols_count, tok_rows) + gate_terms.shape[1:]), axis=1)
    gate_by_vol = jnp.take(gate_sums, slot_vol, axis=0)
    down_part = lax.dot_general(
        act_full, branch_full, (((0,), (0,)), ((), ())), preferred_element_type=jnp.float32
    )
    grad_act = lax.psum_scatter(
        lax.dot_general(
            branch_full, down_weight, (((1,), (1,)), ((), ())), preferred_element_type=jnp.float32
        ).astype(jnp.bfloat16),
        "row",
        scatter_dimension=0,
        tiled=True,
    ).astype(jnp.float32)
    own_down, got_down = pair_send(down_part, "dp", 0)
    grad_hidden = (grad_act * gelu_slope(hidden_own)).astype(jnp.bfloat16)
    grad_full = lax.all_gather(grad_hidden, "row", axis=0, tiled=True)
    got_down, grad_full = lax.optimization_barrier((got_down, grad_full))
    grad_down = own_down + got_down.astype(jnp.float32)
    up_part = lax.dot_general(
        mod_full, grad_full, (((0,), (0,)), ((), ())), preferred_element_type=jnp.float32
    )
    grad_mod_in = slot_scatter_sum(
        lax.dot_general(
            grad_full, up_weight, (((1,), (1,)), ((), ())), preferred_element_type=jnp.float32
        ).astype(jnp.bfloat16),
        "col",
        cols_count,
    )
    grad_norm = grad_mod_in * (1.0 + scale)
    sums = ring_sum(
        jnp.stack([jnp.sum(grad_norm, axis=1), jnp.sum(grad_norm * normed, axis=1)], axis=0),
        "row",
        rows_count,
    )
    first = sums[0] / full_width
    second = sums[1] / full_width
    grad_tokens = cot + rstd[:, None] * (grad_norm - first[:, None] - normed * second[:, None])
    own_grad = jnp.stack([jnp.sum(grad_mod_in, axis=0), jnp.sum(grad_mod_in * normed, axis=0)], axis=0)
    placed = jnp.where(
        (jnp.arange(cols_count, dtype=jnp.int32) == col_index)[:, None, None], own_grad[None], 0.0
    )
    placed = jnp.concatenate([placed, gate_by_vol[:, None, :]], axis=1)
    placed = placed + lax.ppermute(placed, "dp", [(0, 1), (1, 0)])
    far = cols_count // 2
    placed = xor_steps(placed, "col", cols_count, [far])
    up_part, placed = lax.optimization_barrier((up_part, placed))
    near = []
    m = 1
    while m < far:
        near.append(m)
        m *= 2
    grad_mod = xor_steps(placed, "col", cols_count, near)
    own_up, got_up = pair_send(up_part, "dp", 1)
    grad_up = own_up + got_up.astype(jnp.float32)
    cond_f = cond_part.astype(jnp.float32)
    grad_ada = cond_f[0][None, :, None] * grad_mod[0][:, None, :]
    for v in range(1, cols_count):
        grad_ada = grad_ada + cond_f[v][None, :, None] * grad_mod[v][:, None, :]
    return (grad_tokens.astype(jnp.bfloat16), grad_ada, grad_up, grad_down)


def solution(mesh):
    return jax.shard_map(
        body,
        mesh=mesh,
        in_specs=(
            P(("col", "dp"), "row"),
            P(),
            P(None, "col", "row"),
            P("row", "col"),
            P("col", "row"),
            P(("col", "dp"), "row"),
        ),
        out_specs=(
            P(("col", "dp"), "row"),
            P(None, "col", "row"),
            P("row", ("col", "dp")),
            P(("col", "dp"), "row"),
        ),
        check_vma=False,
    )
```

```python
import math

import jax
import jax.numpy as jnp
from jax import lax
from jax.sharding import PartitionSpec as P

tanh_scale = math.sqrt(2.0 / math.pi)


def gelu_tanh(h):
    return 0.5 * h * (1.0 + jnp.tanh(tanh_scale * (h + 0.044715 * h * h * h)))


def gelu_slope(h):
    inner = jnp.tanh(tanh_scale * (h + 0.044715 * h * h * h))
    return 0.5 * (1.0 + inner) + 0.5 * h * (1.0 - inner * inner) * tanh_scale * (
        1.0 + 3.0 * 0.044715 * h * h
    )


def time_features(timesteps, width):
    half = width // 2
    freqs = jnp.exp(-math.log(10000.0) * jnp.arange(half, dtype=jnp.float32) / half)
    angles = timesteps.astype(jnp.float32)[:, None] * freqs[None, :]
    embed = jnp.concatenate([jnp.cos(angles), jnp.sin(angles)], axis=1)
    return jax.nn.silu(embed).astype(jnp.bfloat16)


def shifted(x, axis, n, s):
    return lax.ppermute(x, axis, [(j, (j + s) % n) for j in range(n)])


def slot_gather(x, axis, n):
    return jnp.concatenate([x] + [shifted(x, axis, n, s) for s in range(1, n)], axis=0)


def slot_scatter_sum(parts, axis, n):
    m = parts.shape[0] // n
    total = parts[0:m].astype(jnp.float32)
    for s in range(1, n):
        total = total + shifted(parts[s * m:(s + 1) * m], axis, n, -s).astype(jnp.float32)
    return total


def swapped(x, axis, n, m):
    return lax.ppermute(x, axis, [(j, j ^ m) for j in range(n)])


def ring_sum(x, axis, n):
    m = 1
    while m < n:
        x = x + swapped(x, axis, n, m)
        m *= 2
    return x


def xor_steps(x, axis, n, masks):
    for m in masks:
        x = x + swapped(x, axis, n, m)
    return x


def halving_sum(x, axis, n):
    me = lax.axis_index(axis)
    m = n // 2
    while m >= 1:
        bit = (me // m) % 2
        keep = lax.dynamic_slice_in_dim(x, bit * m, m, 0)
        give = lax.dynamic_slice_in_dim(x, (1 - bit) * m, m, 0)
        x = keep + swapped(give, axis, n, m)
        m //= 2
    return x[0]


def pair_send(part, axis, dim):
    d = lax.axis_index(axis)
    half = part.shape[dim] // 2
    own = lax.dynamic_slice_in_dim(part, d * half, half, dim)
    other = lax.dynamic_slice_in_dim(part, (1 - d) * half, half, dim)
    got = lax.ppermute(other.astype(jnp.bfloat16), axis, [(0, 1), (1, 0)])
    return own, got


def body(tokens, timesteps, ada_weight, up_weight, down_weight, cotangent):
    rows_count = lax.axis_size("row")
    cols_count = lax.axis_size("col")
    col_index = lax.axis_index("col")
    tok_rows, width = tokens.shape
    full_width = width * rows_count
    in_width = ada_weight.shape[1]
    cond = time_features(timesteps, full_width)
    cond_part = lax.dynamic_slice_in_dim(cond, col_index * in_width, in_width, 1)
    mod_terms = jnp.einsum("vi,kio->vko", cond_part, ada_weight, preferred_element_type=jnp.float32)
    mod_all = ring_sum(mod_terms, "col", cols_count)
    own_mod = lax.dynamic_index_in_dim(mod_all, col_index, 0, keepdims=False)
    cot_full = slot_gather(cotangent, "col", cols_count)
    slot_vol = (col_index - jnp.arange(cols_count, dtype=jnp.int32)) % cols_count
    shift = own_mod[0]
    scale = own_mod[1]
    x = tokens.astype(jnp.float32)
    stats = ring_sum(jnp.stack([jnp.sum(x, axis=1), jnp.sum(x * x, axis=1)], axis=0), "row", rows_count)
    mean = stats[0] / full_width
    var = stats[1] / full_width - mean * mean
    rstd = lax.rsqrt(var + 1e-06)
    normed = (x - mean[:, None]) * rstd[:, None]
    modulated = (normed * (1.0 + scale) + shift).astype(jnp.bfloat16)
    cot = cotangent.astype(jnp.float32)
    gate_slots = jnp.take(mod_all[:, 2], slot_vol, axis=0)
    cot_slots = cot_full.astype(jnp.float32).reshape((cols_count, tok_rows, width))
    branch_full = (cot_slots * gate_slots[:, None, :]).astype(jnp.bfloat16).reshape(cot_full.shape)
    mod_full = slot_gather(modulated, "col", cols_count)
    hidden_own = lax.psum_scatter(
        jnp.dot(mod_full, up_weight, preferred_element_type=jnp.float32).astype(jnp.bfloat16),
        "row",
        scatter_dimension=0,
        tiled=True,
    ).astype(jnp.float32)
    act_own = gelu_tanh(hidden_own).astype(jnp.bfloat16)
    act_full = lax.all_gather(act_own, "row", axis=0, tiled=True)
    branch_part = jnp.dot(act_full, down_weight, preferred_element_type=jnp.float32).astype(jnp.bfloat16)
    gate_terms = cot_full.astype(jnp.float32) * branch_part.astype(jnp.float32)
    gate_sums = jnp.sum(gate_terms.reshape((cols_count, tok_rows) + gate_terms.shape[1:]), axis=1)
    gate_by_vol = jnp.take(gate_sums, slot_vol, axis=0)
    down_part = lax.dot_general(
        act_full, branch_full, (((0,), (0,)), ((), ())), preferred_element_type=jnp.float32
    )
    grad_act = lax.psum_scatter(
        lax.dot_general(
            branch_full, down_weight, (((1,), (1,)), ((), ())), preferred_element_type=jnp.float32
        ).astype(jnp.bfloat16),
        "row",
        scatter_dimension=0,
        tiled=True,
    ).astype(jnp.float32)
    own_down, got_down = pair_send(down_part, "dp", 0)
    grad_hidden = (grad_act * gelu_slope(hidden_own)).astype(jnp.bfloat16)
    grad_full = lax.all_gather(grad_hidden, "row", axis=0, tiled=True)
    got_down, grad_full = lax.optimization_barrier((got_down, grad_full))
    grad_down = own_down + got_down.astype(jnp.float32)
    up_part = lax.dot_general(
        mod_full, grad_full, (((0,), (0,)), ((), ())), preferred_element_type=jnp.float32
    )
    grad_mod_in = slot_scatter_sum(
        lax.dot_general(
            grad_full, up_weight, (((1,), (1,)), ((), ())), preferred_element_type=jnp.float32
        ).astype(jnp.bfloat16),
        "col",
        cols_count,
    )
    up_part, grad_mod_in = lax.optimization_barrier((up_part, grad_mod_in))
    own_up, got_up = pair_send(up_part, "dp", 1)
    grad_norm = grad_mod_in * (1.0 + scale)
    sums = ring_sum(
        jnp.stack([jnp.sum(grad_norm, axis=1), jnp.sum(grad_norm * normed, axis=1)], axis=0),
        "row",
        rows_count,
    )
    first = sums[0] / full_width
    second = sums[1] / full_width
    grad_tokens = cot + rstd[:, None] * (grad_norm - first[:, None] - normed * second[:, None])
    own_grad = jnp.stack([jnp.sum(grad_mod_in, axis=0), jnp.sum(grad_mod_in * normed, axis=0)], axis=0)
    placed = jnp.where(
        (jnp.arange(cols_count, dtype=jnp.int32) == col_index)[:, None, None], own_grad[None], 0.0
    )
    placed = jnp.concatenate([placed, gate_by_vol[:, None, :]], axis=1)
    far = cols_count // 2
    masks = [far]
    m = 1
    while m < far:
        masks.append(m)
        m *= 2
    placed = xor_steps(placed, "col", cols_count, masks)
    dp_count = lax.axis_size("dp")
    cross = [
        (c * dp_count + d, (c ^ far) * dp_count + (dp_count - 1 - d))
        for c in range(cols_count)
        for d in range(dp_count)
    ]
    grad_mod = placed + lax.ppermute(placed, ("col", "dp"), cross)
    grad_up = own_up + got_up.astype(jnp.float32)
    cond_f = cond_part.astype(jnp.float32)
    grad_ada = cond_f[0][None, :, None] * grad_mod[0][:, None, :]
    for v in range(1, cols_count):
        grad_ada = grad_ada + cond_f[v][None, :, None] * grad_mod[v][:, None, :]
    return (grad_tokens.astype(jnp.bfloat16), grad_ada, grad_up, grad_down)


def solution(mesh):
    return jax.shard_map(
        body,
        mesh=mesh,
        in_specs=(
            P(("col", "dp"), "row"),
            P(),
            P(None, "col", "row"),
            P("row", "col"),
            P("col", "row"),
            P(("col", "dp"), "row"),
        ),
        out_specs=(
            P(("col", "dp"), "row"),
            P(None, "col", "row"),
            P("row", ("col", "dp")),
            P(("col", "dp"), "row"),
        ),
        check_vma=False,
    )
```

```python
import math

import jax
import jax.numpy as jnp
from jax import lax
from jax.sharding import PartitionSpec as P

tanh_scale = math.sqrt(2.0 / math.pi)


def gelu_tanh(h):
    return 0.5 * h * (1.0 + jnp.tanh(tanh_scale * (h + 0.044715 * h * h * h)))


def gelu_slope(h):
    inner = jnp.tanh(tanh_scale * (h + 0.044715 * h * h * h))
    return 0.5 * (1.0 + inner) + 0.5 * h * (1.0 - inner * inner) * tanh_scale * (
        1.0 + 3.0 * 0.044715 * h * h
    )


def time_features(timesteps, width):
    half = width // 2
    freqs = jnp.exp(-math.log(10000.0) * jnp.arange(half, dtype=jnp.float32) / half)
    angles = timesteps.astype(jnp.float32)[:, None] * freqs[None, :]
    embed = jnp.concatenate([jnp.cos(angles), jnp.sin(angles)], axis=1)
    return jax.nn.silu(embed).astype(jnp.bfloat16)


def shifted(x, axis, n, s):
    return lax.ppermute(x, axis, [(j, (j + s) % n) for j in range(n)])


def slot_gather(x, axis, n):
    return jnp.concatenate([x] + [shifted(x, axis, n, s) for s in range(1, n)], axis=0)


def slot_scatter_sum(parts, axis, n):
    m = parts.shape[0] // n
    total = parts[0:m].astype(jnp.float32)
    for s in range(1, n):
        total = total + shifted(parts[s * m:(s + 1) * m], axis, n, -s).astype(jnp.float32)
    return total


def swapped(x, axis, n, m):
    return lax.ppermute(x, axis, [(j, j ^ m) for j in range(n)])


def ring_sum(x, axis, n):
    m = 1
    while m < n:
        x = x + swapped(x, axis, n, m)
        m *= 2
    return x


def xor_steps(x, axis, n, masks):
    for m in masks:
        x = x + swapped(x, axis, n, m)
    return x


def halving_sum(x, axis, n):
    me = lax.axis_index(axis)
    m = n // 2
    while m >= 1:
        bit = (me // m) % 2
        keep = lax.dynamic_slice_in_dim(x, bit * m, m, 0)
        give = lax.dynamic_slice_in_dim(x, (1 - bit) * m, m, 0)
        x = keep + swapped(give, axis, n, m)
        m //= 2
    return x[0]


def pair_send(part, axis, dim):
    d = lax.axis_index(axis)
    half = part.shape[dim] // 2
    own = lax.dynamic_slice_in_dim(part, d * half, half, dim)
    other = lax.dynamic_slice_in_dim(part, (1 - d) * half, half, dim)
    got = lax.ppermute(other.astype(jnp.bfloat16), axis, [(0, 1), (1, 0)])
    return own, got


def body(tokens, timesteps, ada_weight, up_weight, down_weight, cotangent):
    rows_count = lax.axis_size("row")
    cols_count = lax.axis_size("col")
    col_index = lax.axis_index("col")
    tok_rows, width = tokens.shape
    full_width = width * rows_count
    in_width = ada_weight.shape[1]
    cond = time_features(timesteps, full_width)
    cond_part = lax.dynamic_slice_in_dim(cond, col_index * in_width, in_width, 1)
    mod_terms = jnp.einsum("vi,kio->vko", cond_part, ada_weight, preferred_element_type=jnp.float32)
    mod_all = ring_sum(mod_terms, "col", cols_count)
    own_mod = lax.dynamic_index_in_dim(mod_all, col_index, 0, keepdims=False)
    cot_full = slot_gather(cotangent, "col", cols_count)
    slot_vol = (col_index - jnp.arange(cols_count, dtype=jnp.int32)) % cols_count
    shift = own_mod[0]
    scale = own_mod[1]
    x = tokens.astype(jnp.float32)
    stats = ring_sum(jnp.stack([jnp.sum(x, axis=1), jnp.sum(x * x, axis=1)], axis=0), "row", rows_count)
    mean = stats[0] / full_width
    var = stats[1] / full_width - mean * mean
    rstd = lax.rsqrt(var + 1e-06)
    normed = (x - mean[:, None]) * rstd[:, None]
    modulated = (normed * (1.0 + scale) + shift).astype(jnp.bfloat16)
    cot = cotangent.astype(jnp.float32)
    gate_slots = jnp.take(mod_all[:, 2], slot_vol, axis=0)
    cot_slots = cot_full.astype(jnp.float32).reshape((cols_count, tok_rows, width))
    branch_full = (cot_slots * gate_slots[:, None, :]).astype(jnp.bfloat16).reshape(cot_full.shape)
    mod_full = slot_gather(modulated, "col", cols_count)
    hidden_own = lax.psum_scatter(
        jnp.dot(mod_full, up_weight, preferred_element_type=jnp.float32).astype(jnp.bfloat16),
        "row",
        scatter_dimension=0,
        tiled=True,
    ).astype(jnp.float32)
    act_own = gelu_tanh(hidden_own).astype(jnp.bfloat16)
    normed_src, act_own = lax.optimization_barrier((normed, act_own))
    normed_full = slot_gather(normed_src, "col", cols_count)
    act_full = lax.all_gather(act_own, "row", axis=0, tiled=True)
    normed_full, act_full = lax.optimization_barrier((normed_full, act_full))
    branch_part = jnp.dot(act_full, down_weight, preferred_element_type=jnp.float32).astype(jnp.bfloat16)
    gate_terms = cot_full.astype(jnp.float32) * branch_part.astype(jnp.float32)
    gate_sums = jnp.sum(gate_terms.reshape((cols_count, tok_rows) + gate_terms.shape[1:]), axis=1)
    gate_by_vol = jnp.take(gate_sums, slot_vol, axis=0)
    down_part = lax.dot_general(
        act_full, branch_full, (((0,), (0,)), ((), ())), preferred_element_type=jnp.float32
    )
    grad_act = lax.psum_scatter(
        lax.dot_general(
            branch_full, down_weight, (((1,), (1,)), ((), ())), preferred_element_type=jnp.float32
        ).astype(jnp.bfloat16),
        "row",
        scatter_dimension=0,
        tiled=True,
    ).astype(jnp.float32)
    own_down, got_down = pair_send(down_part, "dp", 0)
    grad_hidden = (grad_act * gelu_slope(hidden_own)).astype(jnp.bfloat16)
    grad_full = lax.all_gather(grad_hidden, "row", axis=0, tiled=True)
    got_down, grad_full = lax.optimization_barrier((got_down, grad_full))
    grad_down = own_down + got_down.astype(jnp.float32)
    up_part = lax.dot_general(
        mod_full, grad_full, (((0,), (0,)), ((), ())), preferred_element_type=jnp.float32
    )
    mod_in_part = lax.dot_general(
        grad_full, up_weight, (((1,), (1,)), ((), ())), preferred_element_type=jnp.float32
    ).astype(jnp.bfloat16)
    part_slots = mod_in_part.astype(jnp.float32).reshape((cols_count, tok_rows, width))
    normed_slots = normed_full.reshape((cols_count, tok_rows, width))
    shift_by_vol = jnp.take(jnp.sum(part_slots, axis=1), slot_vol, axis=0)
    scale_by_vol = jnp.take(jnp.sum(part_slots * normed_slots, axis=1), slot_vol, axis=0)
    grad_mod_in = slot_scatter_sum(mod_in_part, "col", cols_count)
    up_part, grad_mod_in = lax.optimization_barrier((up_part, grad_mod_in))
    own_up, got_up = pair_send(up_part, "dp", 1)
    grad_norm = grad_mod_in * (1.0 + scale)
    sums = ring_sum(
        jnp.stack([jnp.sum(grad_norm, axis=1), jnp.sum(grad_norm * normed, axis=1)], axis=0),
        "row",
        rows_count,
    )
    first = sums[0] / full_width
    second = sums[1] / full_width
    grad_tokens = cot + rstd[:, None] * (grad_norm - first[:, None] - normed * second[:, None])
    placed = jnp.stack([shift_by_vol, scale_by_vol, gate_by_vol], axis=1)
    far = cols_count // 2
    masks = [far]
    m = 1
    while m < far:
        masks.append(m)
        m *= 2
    placed = xor_steps(placed, "col", cols_count, masks)
    dp_count = lax.axis_size("dp")
    cross = [
        (c * dp_count + d, (c ^ far) * dp_count + (dp_count - 1 - d))
        for c in range(cols_count)
        for d in range(dp_count)
    ]
    grad_mod = placed + lax.ppermute(placed, ("col", "dp"), cross)
    grad_up = own_up + got_up.astype(jnp.float32)
    cond_f = cond_part.astype(jnp.float32)
    grad_ada = cond_f[0][None, :, None] * grad_mod[0][:, None, :]
    for v in range(1, cols_count):
        grad_ada = grad_ada + cond_f[v][None, :, None] * grad_mod[v][:, None, :]
    return (grad_tokens.astype(jnp.bfloat16), grad_ada, grad_up, grad_down)


def solution(mesh):
    return jax.shard_map(
        body,
        mesh=mesh,
        in_specs=(
            P(("col", "dp"), "row"),
            P(),
            P(None, "col", "row"),
            P("row", "col"),
            P("col", "row"),
            P(("col", "dp"), "row"),
        ),
        out_specs=(
            P(("col", "dp"), "row"),
            P(None, "col", "row"),
            P("row", ("col", "dp")),
            P(("col", "dp"), "row"),
        ),
        check_vma=False,
    )
```

```python
import math

import jax
import jax.numpy as jnp
from jax import lax
from jax.sharding import PartitionSpec as P

tanh_scale = math.sqrt(2.0 / math.pi)


def gelu_tanh(h):
    return 0.5 * h * (1.0 + jnp.tanh(tanh_scale * (h + 0.044715 * h * h * h)))


def gelu_slope(h):
    inner = jnp.tanh(tanh_scale * (h + 0.044715 * h * h * h))
    return 0.5 * (1.0 + inner) + 0.5 * h * (1.0 - inner * inner) * tanh_scale * (
        1.0 + 3.0 * 0.044715 * h * h
    )


def time_features(timesteps, width):
    half = width // 2
    freqs = jnp.exp(-math.log(10000.0) * jnp.arange(half, dtype=jnp.float32) / half)
    angles = timesteps.astype(jnp.float32)[:, None] * freqs[None, :]
    embed = jnp.concatenate([jnp.cos(angles), jnp.sin(angles)], axis=1)
    return jax.nn.silu(embed).astype(jnp.bfloat16)


def shifted(x, axis, n, s):
    return lax.ppermute(x, axis, [(j, (j + s) % n) for j in range(n)])


def slot_gather(x, axis, n):
    return jnp.concatenate([x] + [shifted(x, axis, n, s) for s in range(1, n)], axis=0)


def slot_scatter_sum(parts, axis, n):
    m = parts.shape[0] // n
    total = parts[0:m].astype(jnp.float32)
    for s in range(1, n):
        total = total + shifted(parts[s * m:(s + 1) * m], axis, n, -s).astype(jnp.float32)
    return total


def swapped(x, axis, n, m):
    return lax.ppermute(x, axis, [(j, j ^ m) for j in range(n)])


def ring_sum(x, axis, n):
    m = 1
    while m < n:
        x = x + swapped(x, axis, n, m)
        m *= 2
    return x


def xor_steps(x, axis, n, masks):
    for m in masks:
        x = x + swapped(x, axis, n, m)
    return x


def halving_sum(x, axis, n):
    me = lax.axis_index(axis)
    m = n // 2
    while m >= 1:
        bit = (me // m) % 2
        keep = lax.dynamic_slice_in_dim(x, bit * m, m, 0)
        give = lax.dynamic_slice_in_dim(x, (1 - bit) * m, m, 0)
        x = keep + swapped(give, axis, n, m)
        m //= 2
    return x[0]


def pair_send(part, axis, dim):
    d = lax.axis_index(axis)
    half = part.shape[dim] // 2
    own = lax.dynamic_slice_in_dim(part, d * half, half, dim)
    other = lax.dynamic_slice_in_dim(part, (1 - d) * half, half, dim)
    got = lax.ppermute(other.astype(jnp.bfloat16), axis, [(0, 1), (1, 0)])
    return own, got


def body(tokens, timesteps, ada_weight, up_weight, down_weight, cotangent):
    rows_count = lax.axis_size("row")
    cols_count = lax.axis_size("col")
    col_index = lax.axis_index("col")
    tok_rows, width = tokens.shape
    full_width = width * rows_count
    in_width = ada_weight.shape[1]
    cond = time_features(timesteps, full_width)
    cond_part = lax.dynamic_slice_in_dim(cond, col_index * in_width, in_width, 1)
    mod_terms = jnp.einsum("vi,kio->vko", cond_part, ada_weight, preferred_element_type=jnp.float32)
    mod_all = ring_sum(mod_terms, "col", cols_count)
    own_mod = lax.dynamic_index_in_dim(mod_all, col_index, 0, keepdims=False)
    cot_full = slot_gather(cotangent, "col", cols_count)
    slot_vol = (col_index - jnp.arange(cols_count, dtype=jnp.int32)) % cols_count
    shift = own_mod[0]
    scale = own_mod[1]
    x = tokens.astype(jnp.float32)
    stats = ring_sum(jnp.stack([jnp.sum(x, axis=1), jnp.sum(x * x, axis=1)], axis=0), "row", rows_count)
    mean = stats[0] / full_width
    var = stats[1] / full_width - mean * mean
    rstd = lax.rsqrt(var + 1e-06)
    normed = (x - mean[:, None]) * rstd[:, None]
    modulated = (normed * (1.0 + scale) + shift).astype(jnp.bfloat16)
    cot = cotangent.astype(jnp.float32)
    gate_slots = jnp.take(mod_all[:, 2], slot_vol, axis=0)
    cot_slots = cot_full.astype(jnp.float32).reshape((cols_count, tok_rows, width))
    branch_full = (cot_slots * gate_slots[:, None, :]).astype(jnp.bfloat16).reshape(cot_full.shape)
    mod_full = slot_gather(modulated, "col", cols_count)
    hidden_own = lax.psum_scatter(
        jnp.dot(mod_full, up_weight, preferred_element_type=jnp.float32).astype(jnp.bfloat16),
        "row",
        scatter_dimension=0,
        tiled=True,
    ).astype(jnp.float32)
    act_own = gelu_tanh(hidden_own).astype(jnp.bfloat16)
    act_full = lax.all_gather(act_own, "row", axis=0, tiled=True)
    branch_part = jnp.dot(act_full, down_weight, preferred_element_type=jnp.float32).astype(jnp.bfloat16)
    gate_terms = cot_full.astype(jnp.float32) * branch_part.astype(jnp.float32)
    gate_sums = jnp.sum(gate_terms.reshape((cols_count, tok_rows) + gate_terms.shape[1:]), axis=1)
    gate_by_vol = jnp.take(gate_sums, slot_vol, axis=0)
    down_part = lax.dot_general(
        act_full, branch_full, (((0,), (0,)), ((), ())), preferred_element_type=jnp.float32
    )
    grad_act = lax.psum_scatter(
        lax.dot_general(
            branch_full, down_weight, (((1,), (1,)), ((), ())), preferred_element_type=jnp.float32
        ).astype(jnp.bfloat16),
        "row",
        scatter_dimension=0,
        tiled=True,
    ).astype(jnp.float32)
    own_down, got_down = pair_send(down_part, "dp", 0)
    grad_hidden = (grad_act * gelu_slope(hidden_own)).astype(jnp.bfloat16)
    grad_full = lax.all_gather(grad_hidden, "row", axis=0, tiled=True)
    got_down, grad_full = lax.optimization_barrier((got_down, grad_full))
    grad_down = own_down + got_down.astype(jnp.float32)
    up_part = lax.dot_general(
        mod_full, grad_full, (((0,), (0,)), ((), ())), preferred_element_type=jnp.float32
    )
    grad_mod_in = slot_scatter_sum(
        lax.dot_general(
            grad_full, up_weight, (((1,), (1,)), ((), ())), preferred_element_type=jnp.float32
        ).astype(jnp.bfloat16),
        "col",
        cols_count,
    )
    own_up, got_up = pair_send(up_part, "dp", 1)
    grad_norm = grad_mod_in * (1.0 + scale)
    sums = ring_sum(
        jnp.stack([jnp.sum(grad_norm, axis=1), jnp.sum(grad_norm * normed, axis=1)], axis=0),
        "row",
        rows_count,
    )
    first = sums[0] / full_width
    second = sums[1] / full_width
    grad_tokens = cot + rstd[:, None] * (grad_norm - first[:, None] - normed * second[:, None])
    own_grad = jnp.stack([jnp.sum(grad_mod_in, axis=0), jnp.sum(grad_mod_in * normed, axis=0)], axis=0)
    placed = jnp.where(
        (jnp.arange(cols_count, dtype=jnp.int32) == col_index)[:, None, None], own_grad[None], 0.0
    )
    placed = jnp.concatenate([placed, gate_by_vol[:, None, :]], axis=1)
    far = cols_count // 2
    masks = [far]
    m = 1
    while m < far:
        masks.append(m)
        m *= 2
    placed = xor_steps(placed, "col", cols_count, masks)
    dp_count = lax.axis_size("dp")
    cross = [
        (c * dp_count + d, (c ^ far) * dp_count + (dp_count - 1 - d))
        for c in range(cols_count)
        for d in range(dp_count)
    ]
    grad_mod = placed + lax.ppermute(placed, ("col", "dp"), cross)
    grad_up = own_up + got_up.astype(jnp.float32)
    cond_f = cond_part.astype(jnp.float32)
    grad_ada = cond_f[0][None, :, None] * grad_mod[0][:, None, :]
    for v in range(1, cols_count):
        grad_ada = grad_ada + cond_f[v][None, :, None] * grad_mod[v][:, None, :]
    return (grad_tokens.astype(jnp.bfloat16), grad_ada, grad_up, grad_down)


def solution(mesh):
    return jax.shard_map(
        body,
        mesh=mesh,
        in_specs=(
            P(("col", "dp"), "row"),
            P(),
            P(None, "col", "row"),
            P("row", "col"),
            P("col", "row"),
            P(("col", "dp"), "row"),
        ),
        out_specs=(
            P(("col", "dp"), "row"),
            P(None, "col", "row"),
            P("row", ("col", "dp")),
            P(("col", "dp"), "row"),
        ),
        check_vma=False,
    )
```

```python
import math

import jax
import jax.numpy as jnp
from jax import lax
from jax.sharding import PartitionSpec as P

tanh_scale = math.sqrt(2.0 / math.pi)


def gelu_tanh(h):
    return 0.5 * h * (1.0 + jnp.tanh(tanh_scale * (h + 0.044715 * h * h * h)))


def gelu_slope(h):
    inner = jnp.tanh(tanh_scale * (h + 0.044715 * h * h * h))
    return 0.5 * (1.0 + inner) + 0.5 * h * (1.0 - inner * inner) * tanh_scale * (
        1.0 + 3.0 * 0.044715 * h * h
    )


def time_features(timesteps, width):
    half = width // 2
    freqs = jnp.exp(-math.log(10000.0) * jnp.arange(half, dtype=jnp.float32) / half)
    angles = timesteps.astype(jnp.float32)[:, None] * freqs[None, :]
    embed = jnp.concatenate([jnp.cos(angles), jnp.sin(angles)], axis=1)
    return jax.nn.silu(embed).astype(jnp.bfloat16)


def shifted(x, axis, n, s):
    return lax.ppermute(x, axis, [(j, (j + s) % n) for j in range(n)])


def slot_gather(x, axis, n):
    return jnp.concatenate([x] + [shifted(x, axis, n, s) for s in range(1, n)], axis=0)


def slot_scatter_sum(parts, axis, n):
    m = parts.shape[0] // n
    total = parts[0:m].astype(jnp.float32)
    for s in range(1, n):
        total = total + shifted(parts[s * m:(s + 1) * m], axis, n, -s).astype(jnp.float32)
    return total


def swapped(x, axis, n, m):
    return lax.ppermute(x, axis, [(j, j ^ m) for j in range(n)])


def ring_sum(x, axis, n):
    m = 1
    while m < n:
        x = x + swapped(x, axis, n, m)
        m *= 2
    return x


def xor_steps(x, axis, n, masks):
    for m in masks:
        x = x + swapped(x, axis, n, m)
    return x


def halving_sum(x, axis, n):
    me = lax.axis_index(axis)
    m = n // 2
    while m >= 1:
        bit = (me // m) % 2
        keep = lax.dynamic_slice_in_dim(x, bit * m, m, 0)
        give = lax.dynamic_slice_in_dim(x, (1 - bit) * m, m, 0)
        x = keep + swapped(give, axis, n, m)
        m //= 2
    return x[0]


def pair_send(part, axis, dim):
    d = lax.axis_index(axis)
    half = part.shape[dim] // 2
    own = lax.dynamic_slice_in_dim(part, d * half, half, dim)
    other = lax.dynamic_slice_in_dim(part, (1 - d) * half, half, dim)
    got = lax.ppermute(other.astype(jnp.bfloat16), axis, [(0, 1), (1, 0)])
    return own, got


def body(tokens, timesteps, ada_weight, up_weight, down_weight, cotangent):
    rows_count = lax.axis_size("row")
    cols_count = lax.axis_size("col")
    col_index = lax.axis_index("col")
    tok_rows, width = tokens.shape
    full_width = width * rows_count
    in_width = ada_weight.shape[1]
    cond = time_features(timesteps, full_width)
    cond_part = lax.dynamic_slice_in_dim(cond, col_index * in_width, in_width, 1)
    mod_terms = jnp.einsum("vi,kio->vko", cond_part, ada_weight, preferred_element_type=jnp.float32)
    mod_all = ring_sum(mod_terms, "col", cols_count)
    own_mod = lax.dynamic_index_in_dim(mod_all, col_index, 0, keepdims=False)
    cot_full = slot_gather(cotangent, "col", cols_count)
    slot_vol = (col_index - jnp.arange(cols_count, dtype=jnp.int32)) % cols_count
    shift = own_mod[0]
    scale = own_mod[1]
    x = tokens.astype(jnp.float32)
    stats = ring_sum(jnp.stack([jnp.sum(x, axis=1), jnp.sum(x * x, axis=1)], axis=0), "row", rows_count)
    mean = stats[0] / full_width
    var = stats[1] / full_width - mean * mean
    rstd = lax.rsqrt(var + 1e-06)
    normed = (x - mean[:, None]) * rstd[:, None]
    modulated = (normed * (1.0 + scale) + shift).astype(jnp.bfloat16)
    cot = cotangent.astype(jnp.float32)
    gate_slots = jnp.take(mod_all[:, 2], slot_vol, axis=0)
    cot_slots = cot_full.astype(jnp.float32).reshape((cols_count, tok_rows, width))
    branch_full = (cot_slots * gate_slots[:, None, :]).astype(jnp.bfloat16).reshape(cot_full.shape)
    mod_full = slot_gather(modulated, "col", cols_count)
    hidden_own = lax.psum_scatter(
        jnp.dot(mod_full, up_weight, preferred_element_type=jnp.float32).astype(jnp.bfloat16),
        "row",
        scatter_dimension=0,
        tiled=True,
    ).astype(jnp.float32)
    act_own = gelu_tanh(hidden_own).astype(jnp.bfloat16)
    act_full = lax.all_gather(act_own, "row", axis=0, tiled=True)
    branch_part = jnp.dot(act_full, down_weight, preferred_element_type=jnp.float32).astype(jnp.bfloat16)
    gate_terms = cot_full.astype(jnp.float32) * branch_part.astype(jnp.float32)
    gate_sums = jnp.sum(gate_terms.reshape((cols_count, tok_rows) + gate_terms.shape[1:]), axis=1)
    gate_by_vol = jnp.take(gate_sums, slot_vol, axis=0)
    down_part = lax.dot_general(
        act_full, branch_full, (((0,), (0,)), ((), ())), preferred_element_type=jnp.float32
    )
    grad_act = lax.psum_scatter(
        lax.dot_general(
            branch_full, down_weight, (((1,), (1,)), ((), ())), preferred_element_type=jnp.float32
        ).astype(jnp.bfloat16),
        "row",
        scatter_dimension=0,
        tiled=True,
    ).astype(jnp.float32)
    own_down, got_down = pair_send(down_part, "dp", 0)
    grad_hidden = (grad_act * gelu_slope(hidden_own)).astype(jnp.bfloat16)
    grad_full = lax.all_gather(grad_hidden, "row", axis=0, tiled=True)
    got_down, grad_full = lax.optimization_barrier((got_down, grad_full))
    grad_down = own_down + got_down.astype(jnp.float32)
    up_part = lax.dot_general(
        mod_full, grad_full, (((0,), (0,)), ((), ())), preferred_element_type=jnp.float32
    )
    grad_mod_in = slot_scatter_sum(
        lax.dot_general(
            grad_full, up_weight, (((1,), (1,)), ((), ())), preferred_element_type=jnp.float32
        ).astype(jnp.bfloat16),
        "col",
        cols_count,
    )
    up_part, grad_mod_in = lax.optimization_barrier((up_part, grad_mod_in))
    own_up, got_up = pair_send(up_part, "dp", 1)
    grad_norm = grad_mod_in * (1.0 + scale)
    sums = ring_sum(
        jnp.stack([jnp.sum(grad_norm, axis=1), jnp.sum(grad_norm * normed, axis=1)], axis=0),
        "row",
        rows_count,
    )
    first = sums[0] / full_width
    second = sums[1] / full_width
    grad_tokens = cot + rstd[:, None] * (grad_norm - first[:, None] - normed * second[:, None])
    own_grad = jnp.stack([jnp.sum(grad_mod_in, axis=0), jnp.sum(grad_mod_in * normed, axis=0)], axis=0)
    placed = jnp.where(
        (jnp.arange(cols_count, dtype=jnp.int32) == col_index)[:, None, None], own_grad[None], 0.0
    )
    placed = jnp.concatenate([placed, gate_by_vol[:, None, :]], axis=1)
    far = cols_count // 2
    masks = []
    m = 1
    while m < far:
        masks.append(m)
        m *= 2
    masks.append(far)
    placed = xor_steps(placed, "col", cols_count, masks)
    dp_count = lax.axis_size("dp")
    cross = [
        (c * dp_count + d, (c ^ far) * dp_count + (dp_count - 1 - d))
        for c in range(cols_count)
        for d in range(dp_count)
    ]
    grad_mod = placed + lax.ppermute(placed, ("col", "dp"), cross)
    grad_up = own_up + got_up.astype(jnp.float32)
    cond_f = cond_part.astype(jnp.float32)
    grad_ada = cond_f[0][None, :, None] * grad_mod[0][:, None, :]
    for v in range(1, cols_count):
        grad_ada = grad_ada + cond_f[v][None, :, None] * grad_mod[v][:, None, :]
    return (grad_tokens.astype(jnp.bfloat16), grad_ada, grad_up, grad_down)


def solution(mesh):
    return jax.shard_map(
        body,
        mesh=mesh,
        in_specs=(
            P(("col", "dp"), "row"),
            P(),
            P(None, "col", "row"),
            P("row", "col"),
            P("col", "row"),
            P(("col", "dp"), "row"),
        ),
        out_specs=(
            P(("col", "dp"), "row"),
            P(None, "col", "row"),
            P("row", ("col", "dp")),
            P(("col", "dp"), "row"),
        ),
        check_vma=False,
    )
```

```python
import math

import jax
import jax.numpy as jnp
from jax import lax
from jax.sharding import PartitionSpec as P

tanh_scale = math.sqrt(2.0 / math.pi)


def gelu_tanh(h):
    return 0.5 * h * (1.0 + jnp.tanh(tanh_scale * (h + 0.044715 * h * h * h)))


def gelu_slope(h):
    inner = jnp.tanh(tanh_scale * (h + 0.044715 * h * h * h))
    return 0.5 * (1.0 + inner) + 0.5 * h * (1.0 - inner * inner) * tanh_scale * (
        1.0 + 3.0 * 0.044715 * h * h
    )


def time_features(timesteps, width):
    half = width // 2
    freqs = jnp.exp(-math.log(10000.0) * jnp.arange(half, dtype=jnp.float32) / half)
    angles = timesteps.astype(jnp.float32)[:, None] * freqs[None, :]
    embed = jnp.concatenate([jnp.cos(angles), jnp.sin(angles)], axis=1)
    return jax.nn.silu(embed).astype(jnp.bfloat16)


def shifted(x, axis, n, s):
    return lax.ppermute(x, axis, [(j, (j + s) % n) for j in range(n)])


def slot_gather(x, axis, n):
    return jnp.concatenate([x] + [shifted(x, axis, n, s) for s in range(1, n)], axis=0)


def slot_scatter_sum(parts, axis, n):
    m = parts.shape[0] // n
    total = parts[0:m].astype(jnp.float32)
    for s in range(1, n):
        total = total + shifted(parts[s * m:(s + 1) * m], axis, n, -s).astype(jnp.float32)
    return total


def swapped(x, axis, n, m):
    return lax.ppermute(x, axis, [(j, j ^ m) for j in range(n)])


def ring_sum(x, axis, n):
    m = 1
    while m < n:
        x = x + swapped(x, axis, n, m)
        m *= 2
    return x


def xor_steps(x, axis, n, masks):
    for m in masks:
        x = x + swapped(x, axis, n, m)
    return x


def halving_sum(x, axis, n):
    me = lax.axis_index(axis)
    m = n // 2
    while m >= 1:
        bit = (me // m) % 2
        keep = lax.dynamic_slice_in_dim(x, bit * m, m, 0)
        give = lax.dynamic_slice_in_dim(x, (1 - bit) * m, m, 0)
        x = keep + swapped(give, axis, n, m)
        m //= 2
    return x[0]


def pair_send(part, axis, dim):
    d = lax.axis_index(axis)
    half = part.shape[dim] // 2
    own = lax.dynamic_slice_in_dim(part, d * half, half, dim)
    other = lax.dynamic_slice_in_dim(part, (1 - d) * half, half, dim)
    got = lax.ppermute(other.astype(jnp.bfloat16), axis, [(0, 1), (1, 0)])
    return own, got


def body(tokens, timesteps, ada_weight, up_weight, down_weight, cotangent):
    rows_count = lax.axis_size("row")
    cols_count = lax.axis_size("col")
    col_index = lax.axis_index("col")
    tok_rows, width = tokens.shape
    full_width = width * rows_count
    in_width = ada_weight.shape[1]
    cond = time_features(timesteps, full_width)
    cond_part = lax.dynamic_slice_in_dim(cond, col_index * in_width, in_width, 1)
    mod_terms = jnp.einsum("vi,kio->vko", cond_part, ada_weight, preferred_element_type=jnp.float32)
    mod_all = ring_sum(mod_terms, "col", cols_count)
    own_mod = lax.dynamic_index_in_dim(mod_all, col_index, 0, keepdims=False)
    cot_full = slot_gather(cotangent, "col", cols_count)
    slot_vol = (col_index - jnp.arange(cols_count, dtype=jnp.int32)) % cols_count
    shift = own_mod[0]
    scale = own_mod[1]
    x = tokens.astype(jnp.float32)
    stats = ring_sum(jnp.stack([jnp.sum(x, axis=1), jnp.sum(x * x, axis=1)], axis=0), "row", rows_count)
    mean = stats[0] / full_width
    var = stats[1] / full_width - mean * mean
    rstd = lax.rsqrt(var + 1e-06)
    normed = (x - mean[:, None]) * rstd[:, None]
    modulated = (normed * (1.0 + scale) + shift).astype(jnp.bfloat16)
    cot = cotangent.astype(jnp.float32)
    gate_slots = jnp.take(mod_all[:, 2], slot_vol, axis=0)
    cot_slots = cot_full.astype(jnp.float32).reshape((cols_count, tok_rows, width))
    branch_full = (cot_slots * gate_slots[:, None, :]).astype(jnp.bfloat16).reshape(cot_full.shape)
    mod_full = slot_gather(modulated, "col", cols_count)
    hidden_own = lax.psum_scatter(
        jnp.dot(mod_full, up_weight, preferred_element_type=jnp.float32).astype(jnp.bfloat16),
        "row",
        scatter_dimension=0,
        tiled=True,
    ).astype(jnp.float32)
    act_own = gelu_tanh(hidden_own).astype(jnp.bfloat16)
    act_full = lax.all_gather(act_own, "row", axis=0, tiled=True)
    branch_part = jnp.dot(act_full, down_weight, preferred_element_type=jnp.float32).astype(jnp.bfloat16)
    gate_terms = cot_full.astype(jnp.float32) * branch_part.astype(jnp.float32)
    gate_sums = jnp.sum(gate_terms.reshape((cols_count, tok_rows) + gate_terms.shape[1:]), axis=1)
    gate_by_vol = jnp.take(gate_sums, slot_vol, axis=0)
    down_part = lax.dot_general(
        act_full, branch_full, (((0,), (0,)), ((), ())), preferred_element_type=jnp.float32
    )
    grad_act = lax.psum_scatter(
        lax.dot_general(
            branch_full, down_weight, (((1,), (1,)), ((), ())), preferred_element_type=jnp.float32
        ).astype(jnp.bfloat16),
        "row",
        scatter_dimension=0,
        tiled=True,
    ).astype(jnp.float32)
    own_down, got_down = pair_send(down_part, "dp", 0)
    grad_hidden = (grad_act * gelu_slope(hidden_own)).astype(jnp.bfloat16)
    grad_full = lax.all_gather(grad_hidden, "row", axis=0, tiled=True)
    got_down, grad_full = lax.optimization_barrier((got_down, grad_full))
    grad_down = own_down + got_down.astype(jnp.float32)
    grad_mod_in = slot_scatter_sum(
        lax.dot_general(
            grad_full, up_weight, (((1,), (1,)), ((), ())), preferred_element_type=jnp.float32
        ).astype(jnp.bfloat16),
        "col",
        cols_count,
    )
    up_rows, grad_mod_in = lax.optimization_barrier((grad_full, grad_mod_in))
    up_part = lax.dot_general(
        mod_full, up_rows, (((0,), (0,)), ((), ())), preferred_element_type=jnp.float32
    )
    own_up, got_up = pair_send(up_part, "dp", 1)
    grad_norm = grad_mod_in * (1.0 + scale)
    sums = ring_sum(
        jnp.stack([jnp.sum(grad_norm, axis=1), jnp.sum(grad_norm * normed, axis=1)], axis=0),
        "row",
        rows_count,
    )
    first = sums[0] / full_width
    second = sums[1] / full_width
    grad_tokens = cot + rstd[:, None] * (grad_norm - first[:, None] - normed * second[:, None])
    own_grad = jnp.stack([jnp.sum(grad_mod_in, axis=0), jnp.sum(grad_mod_in * normed, axis=0)], axis=0)
    placed = jnp.where(
        (jnp.arange(cols_count, dtype=jnp.int32) == col_index)[:, None, None], own_grad[None], 0.0
    )
    placed = jnp.concatenate([placed, gate_by_vol[:, None, :]], axis=1)
    far = cols_count // 2
    masks = [far]
    m = 1
    while m < far:
        masks.append(m)
        m *= 2
    placed = xor_steps(placed, "col", cols_count, masks)
    dp_count = lax.axis_size("dp")
    cross = [
        (c * dp_count + d, (c ^ far) * dp_count + (dp_count - 1 - d))
        for c in range(cols_count)
        for d in range(dp_count)
    ]
    grad_mod = placed + lax.ppermute(placed, ("col", "dp"), cross)
    grad_up = own_up + got_up.astype(jnp.float32)
    cond_f = cond_part.astype(jnp.float32)
    grad_ada = cond_f[0][None, :, None] * grad_mod[0][:, None, :]
    for v in range(1, cols_count):
        grad_ada = grad_ada + cond_f[v][None, :, None] * grad_mod[v][:, None, :]
    return (grad_tokens.astype(jnp.bfloat16), grad_ada, grad_up, grad_down)


def solution(mesh):
    return jax.shard_map(
        body,
        mesh=mesh,
        in_specs=(
            P(("col", "dp"), "row"),
            P(),
            P(None, "col", "row"),
            P("row", "col"),
            P("col", "row"),
            P(("col", "dp"), "row"),
        ),
        out_specs=(
            P(("col", "dp"), "row"),
            P(None, "col", "row"),
            P("row", ("col", "dp")),
            P(("col", "dp"), "row"),
        ),
        check_vma=False,
    )
```
